128 devices in a mesh: tok: 16 (over x, y), voc: 8 (over z, core).
Axes of the slice: x: 4, y: 4, z: 4, core: 2. Of those that a mesh axis runs over, the one named last changes fastest.
Arguments:
- hidden_rows: bfloat16 [512, 3584], P(('tok', 'voc')), may hold values from -40 to 40
- head_weight: bfloat16 [147456, 3584], P(('tok', 'voc')), may hold values from -0.09375 to 0.09375
- teacher_index: int32 [512, 64], replicated, may hold values from 0 to 147455, as said below
- teacher_logprob: float32 [512, 64], replicated, may hold values from -10 to -4.2
Outputs:
- row_loss: float32 [512], P(('tok', 'voc'))
- head_grad: bfloat16 [147456, 3584], P(('tok', 'voc'))
- input_grad: bfloat16 [512, 3584], P(('tok', 'voc'))
The draws below stay inside these ranges and needn't reach their ends.
Inputs may be any that keep to these rules, and one draw needn't show every extreme that they name: `teacher_index`: the 64 entries of one token are distinct.
All inputs are finite; a program needn't handle non-finite values.
Results may differ from the reference program's by a relative error of at most 0.015.
Values may be sent and summed in bfloat16 or wider, within the bound.
No kernel may reach another device: no remote copies, remote signals or barrier semaphores. Data moves between devices by JAX's collectives and lax.ppermute only.
A program may use at most 128 MiB of HBM per device.

```python
import jax
import jax.numpy as jnp
from jax import lax

D = 3584
VOC_DEV = 1152
TOPK = 64
V = 147456
TOKENS = 512


def head_values(key):
    values = jax.random.normal(jax.random.fold_in(key, 11), (V, D), jnp.float32) * D ** (-0.5)
    return jnp.clip(values, -0.09375, 0.09375)


def draw_head_weight(key, part):
    return head_values(key).astype(jnp.bfloat16)


def draw_hidden_rows(key, part):
    scales = jnp.exp(jax.random.uniform(jax.random.fold_in(key, 31), (TOKENS, 1), jnp.float32, 0.0, 2.0794))
    weights = head_values(key)
    first = jax.random.randint(jax.random.fold_in(key, 41), (TOKENS,), 0, V)
    second = jax.random.randint(jax.random.fold_in(key, 43), (TOKENS,), 0, V)
    strength = jax.random.uniform(jax.random.fold_in(key, 47), (TOKENS, 1), jnp.float32, 60.0, 300.0)
    gap = jax.random.uniform(jax.random.fold_in(key, 53), (TOKENS, 1), jnp.float32, 1.0, 3.0)
    aligned = strength * weights[first] + (strength - gap) * weights[second]
    chosen = jax.random.randint(jax.random.fold_in(key, 59), (TOKENS, 1), 0, 6) == 0
    gauss = jax.random.normal(jax.random.fold_in(key, 23), (TOKENS, D), jnp.float32)
    base = gauss * scales
    values = jnp.where(chosen, aligned, base)
    return jnp.clip(values, -40.0, 40.0).astype(jnp.bfloat16)


def draw_teacher_index(key, part):
    span = V - TOPK + 1
    draws = jax.random.randint(jax.random.fold_in(key, 61), (TOKENS, TOPK), 0, span)
    draws = draws.at[0, 0].set(span - 1).at[1, 0].set(0)
    steps = jnp.arange(TOPK, dtype=jnp.int32)[None, :]
    ordered = jnp.sort(draws, axis=1) + steps
    keys = jax.random.randint(jax.random.fold_in(key, 67), (TOKENS, TOPK), 0, 65536) * TOPK + steps
    order = jnp.argsort(keys, axis=1)
    return jnp.take_along_axis(ordered, order, axis=1).astype(jnp.int32)


def setup_inputs(seed: int = 0) -> dict:
    seeds = jax.random.split(jax.random.key(seed), 5)
    hidden_rows = draw_hidden_rows(jax.random.fold_in(seeds[4], 71), 0)
    head_weight = draw_head_weight(jax.random.fold_in(seeds[4], 71), 0)
    teacher_index = draw_teacher_index(jax.random.fold_in(seeds[4], 71), 0)
    teacher_logprob = jnp.clip(jax.random.uniform(seeds[3], (TOKENS, TOPK), jnp.float32, -10.0, -4.2), -10.0, -4.2)
    return {"hidden_rows": hidden_rows, "head_weight": head_weight, "teacher_index": teacher_index, "teacher_logprob": teacher_logprob}


loss_scale = 256.0


def reference(hidden_rows, head_weight, teacher_index, teacher_logprob):
    blocks = TOKENS // 64
    hid_b = hidden_rows.reshape(blocks, 64, D)
    idx_b = teacher_index.reshape(blocks, 64, TOPK)
    lp_b = teacher_logprob.reshape(blocks, 64, TOPK)

    def one_block(args):
        rows, index, logprob = args
        logits = jnp.dot(rows, head_weight.T, preferred_element_type=jnp.float32)
        peak = jnp.max(logits, axis=1)
        lse = peak + jnp.log(jnp.sum(jnp.exp(logits - peak[:, None]), axis=1))
        probs = jnp.exp(logprob)
        total_p = jnp.sum(probs, axis=1)
        picked = jnp.take_along_axis(logits, index, axis=1)
        loss = jnp.sum(probs * (logprob - picked + lse[:, None]), axis=1)
        rowpos = jnp.broadcast_to(jnp.arange(64, dtype=jnp.int32)[:, None], index.shape)
        target = jnp.zeros(logits.shape, jnp.float32).at[rowpos, index].add(probs)
        grad = (loss_scale * (total_p[:, None] * jnp.exp(logits - lse[:, None]) - target)).astype(jnp.bfloat16)
        return grad, loss

    grad_b, loss_b = lax.map(one_block, (hid_b, idx_b, lp_b))
    grad = grad_b.reshape(TOKENS, V)
    row_loss = loss_b.reshape(TOKENS)
    count = V // VOC_DEV

    def head_block(block):
        piece = lax.dynamic_slice_in_dim(grad, (block * VOC_DEV).astype(jnp.int32), VOC_DEV, 1)
        return lax.dot_general(piece, hidden_rows, (((0,), (0,)), ((), ())), preferred_element_type=jnp.float32).astype(jnp.bfloat16)

    head_grad = lax.map(head_block, jnp.arange(count, dtype=jnp.int32)).reshape(V, D)
    input_grad = jnp.dot(grad, head_weight, preferred_element_type=jnp.float32).astype(jnp.bfloat16)
    return row_loss, head_grad, input_grad
```

```python
import jax
import jax.numpy as jnp
from jax import lax
from jax.sharding import PartitionSpec as P

loss_scale = 256.0
RING = 4


def teacher_target(local, probs, voc_dev):
    blocks = local.shape[0] // 64
    local_b = local.reshape(blocks, 64, local.shape[1])
    probs_b = probs.reshape(blocks, 64, probs.shape[1])
    columns = jnp.arange(voc_dev, dtype=jnp.int32)[None, None, :]

    def one_block(args):
        block_local, block_probs = args
        equal = block_local[:, :, None] == columns
        return jnp.sum(jnp.where(equal, block_probs[:, :, None], 0.0), axis=1)

    return lax.map(one_block, (local_b, probs_b)).reshape(local.shape[0], voc_dev)


def coords():
    tok = lax.axis_index("tok")
    voc = lax.axis_index("voc")
    return {"x": tok // RING, "y": tok % RING, "z": voc // 2, "c": voc % 2}


def stage_pairs(stage, shift, tok_n, voc_n):
    if stage == "c":
        return "voc", [(v, v ^ 1) for v in range(voc_n)]
    if stage == "z":
        return "voc", [(v, ((v // 2 + shift) % RING) * 2 + v % 2) for v in range(voc_n)]
    if stage == "y":
        return "tok", [(t, (t // RING) * RING + (t % RING + shift) % RING) for t in range(tok_n)]
    return "tok", [(t, ((t // RING + shift) % RING) * RING + t % RING) for t in range(tok_n)]


def exchange(block_for, stage, me, tok_n, voc_n, ordered):
    n = 2 if stage == "c" else RING
    got = []
    for shift in range(n):
        if shift == 0:
            got.append(block_for(me))
            continue
        axis, pairs = stage_pairs(stage, shift, tok_n, voc_n)
        target = (me ^ 1) if stage == "c" else (me + shift) % RING
        got.append(lax.ppermute(block_for(target), axis, pairs))
    stacked = jnp.stack(got)
    if not ordered:
        return stacked
    if stage == "c":
        order = jnp.arange(2, dtype=jnp.int32) ^ me
    else:
        order = (me - jnp.arange(RING, dtype=jnp.int32)) % RING
    return jnp.take(stacked, order, axis=0)


def per_device(hidden_rows, head_weight, teacher_index, teacher_logprob, tok_n, voc_n):
    voc_dev = head_weight.shape[0]
    tok_dev = hidden_rows.shape[0]
    width = hidden_rows.shape[1]
    at = coords()

    every = hidden_rows
    for stage, axis in (("x", 0), ("y", 1), ("z", 2), ("c", 3)):
        got = exchange(lambda k: every, stage, at[stage], tok_n, voc_n, True)
        every = jnp.moveaxis(got, 0, axis)
    every = every.reshape(-1, width)

    logits = lax.dot_general(
        every, head_weight, (((1,), (1,)), ((), ())), preferred_element_type=jnp.float32
    )
    position = lax.axis_index(("tok", "voc"))
    offset = position * voc_dev
    local = teacher_index - offset
    probs = jnp.exp(teacher_logprob)
    target = teacher_target(local, probs, voc_dev)
    part_dot = jnp.sum(logits * target, axis=1)
    local_peak = jnp.max(logits, axis=1)
    local_sum = jnp.sum(jnp.exp(logits - local_peak[:, None]), axis=1)

    stats = jnp.stack([local_peak, local_sum, part_dot])
    for stage in ("c", "z", "y", "x"):
        got = exchange(lambda k: stats, stage, at[stage], tok_n, voc_n, True)
        peak = jnp.max(got[:, 0], axis=0)
        summed = jnp.sum(got[:, 1] * jnp.exp(got[:, 0] - peak[None]), axis=0)
        dotted = jnp.sum(got[:, 2], axis=0)
        stats = jnp.stack([peak, summed, dotted])
    peak, summed, dotted = stats[0], stats[1], stats[2]

    lse = peak + jnp.log(summed)
    total_p = jnp.sum(probs, axis=1)
    own_term = jnp.sum(probs * teacher_logprob, axis=1)
    loss_all = own_term - dotted + total_p * lse
    row_loss = lax.dynamic_slice_in_dim(loss_all, position * tok_dev, tok_dev, 0)
    grad = (loss_scale * (total_p[:, None] * jnp.exp(logits - lse[:, None]) - target)).astype(
        jnp.bfloat16
    )
    partial = jnp.dot(grad, head_weight, preferred_element_type=jnp.float32)
    head_grad = lax.dot_general(
        grad, every, (((0,), (0,)), ((), ())), preferred_element_type=jnp.float32
    ).astype(jnp.bfloat16)

    part = partial.reshape(RING, RING, RING, 2, tok_dev, width)
    got = exchange(
        lambda k: lax.dynamic_index_in_dim(part, k, 3, keepdims=False).astype(jnp.bfloat16),
        "c", at["c"], tok_n, voc_n, False,
    )
    acc = jnp.sum(got.astype(jnp.float32), axis=0)
    got = exchange(
        lambda k: lax.dynamic_index_in_dim(acc, k, 2, keepdims=False).astype(jnp.bfloat16),
        "z", at["z"], tok_n, voc_n, False,
    )
    acc = jnp.sum(got.astype(jnp.float32), axis=0)
    got = exchange(
        lambda k: lax.dynamic_index_in_dim(acc, k, 1, keepdims=False).astype(jnp.bfloat16),
        "y", at["y"], tok_n, voc_n, False,
    )
    acc = jnp.sum(got.astype(jnp.float32), axis=0)
    got = exchange(
        lambda k: lax.dynamic_index_in_dim(acc, k, 0, keepdims=False).astype(jnp.bfloat16),
        "x", at["x"], tok_n, voc_n, False,
    )
    input_sum = jnp.sum(got.astype(jnp.float32), axis=0)
    return (row_loss, head_grad, input_sum.astype(jnp.bfloat16))


def solution(mesh):
    tok_n = mesh.shape["tok"]
    voc_n = mesh.shape["voc"]
    placed = (P(("tok", "voc"), None), P(("tok", "voc"), None), P(), P())

    def body(h, w, ti, tl):
        return per_device(h, w, ti, tl, tok_n, voc_n)

    return jax.shard_map(
        body,
        mesh=mesh,
        in_specs=placed,
        out_specs=(P(("tok", "voc")), P(("tok", "voc"), None), P(("tok", "voc"), None)),
        check_vma=False,
    )
```

```python
import jax
import jax.numpy as jnp
from jax import lax
from jax.sharding import PartitionSpec as P

loss_scale = 256.0
RING = 4


def coords():
    tok = lax.axis_index("tok")
    voc = lax.axis_index("voc")
    return {"x": tok // RING, "y": tok % RING, "z": voc // 2, "c": voc % 2}


def stage_pairs(stage, shift, tok_n, voc_n):
    if stage == "c":
        return "voc", [(v, v ^ 1) for v in range(voc_n)]
    if stage == "z":
        return "voc", [(v, ((v // 2 + shift) % RING) * 2 + v % 2) for v in range(voc_n)]
    if stage == "y":
        return "tok", [(t, (t // RING) * RING + (t % RING + shift) % RING) for t in range(tok_n)]
    return "tok", [(t, ((t // RING + shift) % RING) * RING + t % RING) for t in range(tok_n)]


def exchange(block_for, stage, tok_n, voc_n):
    n = 2 if stage == "c" else RING
    got = [block_for(0)]
    for shift in range(1, n):
        axis, pairs = stage_pairs(stage, shift, tok_n, voc_n)
        got.append(lax.ppermute(block_for(shift), axis, pairs))
    return jnp.stack(got)


def ring_order(me, n):
    if n == 2:
        return jnp.arange(2, dtype=jnp.int32) ^ me
    return (me - jnp.arange(n, dtype=jnp.int32)) % n


def to_arrival(nat, at):
    rest = nat.shape[1:]
    a = nat.reshape((RING, RING, RING, 2, -1) + rest)
    for axis, stage, n in ((0, "x", RING), (1, "y", RING), (2, "z", RING), (3, "c", 2)):
        a = jnp.take(a, ring_order(at[stage], n), axis=axis)
    a = jnp.transpose(a, (3, 2, 1, 0) + tuple(range(4, a.ndim)))
    return a.reshape(nat.shape)


def to_natural(arr, at):
    lead = arr.shape[:-1]
    k = len(lead)
    a = arr.reshape(lead + (2, RING, RING, RING, -1))
    for axis, stage, n in ((k, "c", 2), (k + 1, "z", RING), (k + 2, "y", RING), (k + 3, "x", RING)):
        a = jnp.take(a, ring_order(at[stage], n), axis=axis)
    perm = tuple(range(k)) + (k + 3, k + 2, k + 1, k, k + 4)
    return jnp.transpose(a, perm).reshape(arr.shape)


def per_device(hidden_rows, head_weight, teacher_index, teacher_logprob, tok_n, voc_n):
    voc_dev = head_weight.shape[0]
    tok_dev = hidden_rows.shape[0]
    width = hidden_rows.shape[1]
    at = coords()

    every = hidden_rows
    for stage in ("x", "y", "z", "c"):
        got = exchange(lambda s: every, stage, tok_n, voc_n)
        every = got.reshape(-1, width)

    logits = lax.dot_general(
        every, head_weight, (((1,), (1,)), ((), ())), preferred_element_type=jnp.float32
    )
    position = lax.axis_index(("tok", "voc"))
    offset = position * voc_dev
    index_arr = to_arrival(teacher_index, at)
    logprob_arr = to_arrival(teacher_logprob, at)
    local = index_arr - offset
    probs_arr = jnp.exp(logprob_arr)
    columns = jnp.arange(voc_dev, dtype=jnp.int32)[None, None, :]
    target = jnp.sum(jnp.where(local[:, :, None] == columns, probs_arr[:, :, None], 0.0), axis=1)
    part_dot = jnp.sum(logits * target, axis=1)
    local_peak = jnp.max(logits, axis=1)
    local_sum = jnp.sum(jnp.exp(logits - local_peak[:, None]), axis=1)

    stats = to_natural(jnp.stack([local_peak, local_sum, part_dot]), at)
    for stage in ("c", "z", "y", "x"):
        n = 2 if stage == "c" else RING
        got = exchange(lambda s: stats, stage, tok_n, voc_n)
        got = jnp.take(got, ring_order(at[stage], n), axis=0)
        peak = jnp.max(got[:, 0], axis=0)
        summed = jnp.sum(got[:, 1] * jnp.exp(got[:, 0] - peak[None]), axis=0)
        dotted = jnp.sum(got[:, 2], axis=0)
        stats = jnp.stack([peak, summed, dotted])
    peak, summed, dotted = stats[0], stats[1], stats[2]

    lse = peak + jnp.log(summed)
    probs = jnp.exp(teacher_logprob)
    total_p = jnp.sum(probs, axis=1)
    own_term = jnp.sum(probs * teacher_logprob, axis=1)
    loss_all = own_term - dotted + total_p * lse
    row_loss = lax.dynamic_slice_in_dim(loss_all, position * tok_dev, tok_dev, 0)
    lse_arr = to_arrival(lse, at)
    total_arr = jnp.sum(probs_arr, axis=1)
    grad = (loss_scale * (total_arr[:, None] * jnp.exp(logits - lse_arr[:, None]) - target)).astype(
        jnp.bfloat16
    )
    partial = jnp.dot(grad, head_weight, preferred_element_type=jnp.float32)
    head_grad = lax.dot_general(
        grad, every, (((0,), (0,)), ((), ())), preferred_element_type=jnp.float32
    ).astype(jnp.bfloat16)

    acc = partial.reshape(2, -1, width)
    for stage in ("c", "z", "y", "x"):
        n = acc.shape[0]
        got = exchange(lambda s: acc[(-s) % n].astype(jnp.bfloat16), stage, tok_n, voc_n)
        acc = acc[0] + jnp.sum(got[1:].astype(jnp.float32), axis=0)
        if stage != "x":
            acc = acc.reshape(RING, -1, width)
    return (row_loss, head_grad, acc.astype(jnp.bfloat16))


def solution(mesh):
    tok_n = mesh.shape["tok"]
    voc_n = mesh.shape["voc"]
    placed = (P(("tok", "voc"), None), P(("tok", "voc"), None), P(), P())

    def body(h, w, ti, tl):
        return per_device(h, w, ti, tl, tok_n, voc_n)

    return jax.shard_map(
        body,
        mesh=mesh,
        in_specs=placed,
        out_specs=(P(("tok", "voc")), P(("tok", "voc"), None), P(("tok", "voc"), None)),
        check_vma=False,
    )
```

```python
import jax
import jax.numpy as jnp
from jax import lax
from jax.sharding import PartitionSpec as P

loss_scale = 256.0
RING = 4


HITS = 8


def dense_target(local, probs, voc_dev):
    blocks = local.shape[0] // 64
    local_b = local.reshape(blocks, 64, local.shape[1])
    probs_b = probs.reshape(blocks, 64, probs.shape[1])
    columns = jnp.arange(voc_dev, dtype=jnp.int32)[None, None, :]

    def one_block(args):
        block_local, block_probs = args
        equal = block_local[:, :, None] == columns
        return jnp.sum(jnp.where(equal, block_probs[:, :, None], 0.0), axis=1)

    return lax.map(one_block, (local_b, probs_b)).reshape(local.shape[0], voc_dev)


def compact_target(local, probs, voc_dev):
    valid = (local >= 0) & (local < voc_dev)
    rank = jnp.cumsum(valid.astype(jnp.int32), axis=1) - 1
    slot = jnp.arange(HITS, dtype=jnp.int32)[None, None, :]
    chosen = valid[:, :, None] & (rank[:, :, None] == slot)
    slot_local = jnp.sum(jnp.where(chosen, local[:, :, None], 0), axis=1)
    slot_probs = jnp.sum(jnp.where(chosen, probs[:, :, None], 0.0), axis=1)
    columns = jnp.arange(voc_dev, dtype=jnp.int32)[None, :]
    target = jnp.zeros((local.shape[0], voc_dev), jnp.float32)
    for j in range(HITS):
        target = target + jnp.where(slot_local[:, j : j + 1] == columns, slot_probs[:, j : j + 1], 0.0)
    return target


def teacher_target(local, probs, voc_dev):
    valid = (local >= 0) & (local < voc_dev)
    crowded = jnp.any(jnp.sum(valid.astype(jnp.int32), axis=1) > HITS)
    return lax.cond(
        crowded,
        lambda: dense_target(local, probs, voc_dev),
        lambda: compact_target(local, probs, voc_dev),
    )


def coords():
    tok = lax.axis_index("tok")
    voc = lax.axis_index("voc")
    return {"x": tok // RING, "y": tok % RING, "z": voc // 2, "c": voc % 2}


def stage_pairs(stage, shift, tok_n, voc_n):
    if stage == "c":
        return "voc", [(v, v ^ 1) for v in range(voc_n)]
    if stage == "z":
        return "voc", [(v, ((v // 2 + shift) % RING) * 2 + v % 2) for v in range(voc_n)]
    if stage == "y":
        return "tok", [(t, (t // RING) * RING + (t % RING + shift) % RING) for t in range(tok_n)]
    return "tok", [(t, ((t // RING + shift) % RING) * RING + t % RING) for t in range(tok_n)]


def exchange(block_for, stage, tok_n, voc_n):
    n = 2 if stage == "c" else RING
    got = [block_for(0)]
    for shift in range(1, n):
        axis, pairs = stage_pairs(stage, shift, tok_n, voc_n)
        got.append(lax.ppermute(block_for(shift), axis, pairs))
    return jnp.stack(got)


def ring_order(me, n):
    if n == 2:
        return jnp.arange(2, dtype=jnp.int32) ^ me
    return (me - jnp.arange(n, dtype=jnp.int32)) % n


def to_arrival(nat, at):
    rest = nat.shape[1:]
    a = nat.reshape((RING, RING, RING, 2, -1) + rest)
    for axis, stage, n in ((0, "x", RING), (1, "y", RING), (2, "z", RING), (3, "c", 2)):
        a = jnp.take(a, ring_order(at[stage], n), axis=axis)
    a = jnp.transpose(a, (3, 2, 1, 0) + tuple(range(4, a.ndim)))
    return a.reshape(nat.shape)


def to_natural(arr, at):
    lead = arr.shape[:-1]
    k = len(lead)
    a = arr.reshape(lead + (2, RING, RING, RING, -1))
    for axis, stage, n in ((k, "c", 2), (k + 1, "z", RING), (k + 2, "y", RING), (k + 3, "x", RING)):
        a = jnp.take(a, ring_order(at[stage], n), axis=axis)
    perm = tuple(range(k)) + (k + 3, k + 2, k + 1, k, k + 4)
    return jnp.transpose(a, perm).reshape(arr.shape)


def per_device(hidden_rows, head_weight, teacher_index, teacher_logprob, tok_n, voc_n):
    voc_dev = head_weight.shape[0]
    tok_dev = hidden_rows.shape[0]
    width = hidden_rows.shape[1]
    at = coords()

    every = hidden_rows
    for stage in ("x", "y", "z", "c"):
        got = exchange(lambda s: every, stage, tok_n, voc_n)
        every = got.reshape(-1, width)

    logits = lax.dot_general(
        every, head_weight, (((1,), (1,)), ((), ())), preferred_element_type=jnp.float32
    )
    position = lax.axis_index(("tok", "voc"))
    offset = position * voc_dev
    index_arr = to_arrival(teacher_index, at)
    logprob_arr = to_arrival(teacher_logprob, at)
    local = index_arr - offset
    probs_arr = jnp.exp(logprob_arr)
    target = teacher_target(local, probs_arr, voc_dev)
    part_dot = jnp.sum(logits * target, axis=1)
    local_peak = jnp.max(logits, axis=1)
    local_sum = jnp.sum(jnp.exp(logits - local_peak[:, None]), axis=1)

    stats = to_natural(jnp.stack([local_peak, local_sum, part_dot]), at)
    for stage in ("c", "z", "y", "x"):
        n = 2 if stage == "c" else RING
        got = exchange(lambda s: stats, stage, tok_n, voc_n)
        got = jnp.take(got, ring_order(at[stage], n), axis=0)
        peak = jnp.max(got[:, 0], axis=0)
        summed = jnp.sum(got[:, 1] * jnp.exp(got[:, 0] - peak[None]), axis=0)
        dotted = jnp.sum(got[:, 2], axis=0)
        stats = jnp.stack([peak, summed, dotted])
    peak, summed, dotted = stats[0], stats[1], stats[2]

    lse = peak + jnp.log(summed)
    probs = jnp.exp(teacher_logprob)
    total_p = jnp.sum(probs, axis=1)
    own_term = jnp.sum(probs * teacher_logprob, axis=1)
    loss_all = own_term - dotted + total_p * lse
    row_loss = lax.dynamic_slice_in_dim(loss_all, position * tok_dev, tok_dev, 0)
    lse_arr = to_arrival(lse, at)
    total_arr = jnp.sum(probs_arr, axis=1)
    grad = (loss_scale * (total_arr[:, None] * jnp.exp(logits - lse_arr[:, None]) - target)).astype(
        jnp.bfloat16
    )
    partial = jnp.dot(grad, head_weight, preferred_element_type=jnp.float32)
    head_grad = lax.dot_general(
        grad, every, (((0,), (0,)), ((), ())), preferred_element_type=jnp.float32
    ).astype(jnp.bfloat16)

    acc = partial.reshape(2, -1, width)
    for stage in ("c", "z", "y", "x"):
        n = acc.shape[0]
        got = exchange(lambda s: acc[(-s) % n].astype(jnp.bfloat16), stage, tok_n, voc_n)
        acc = acc[0] + jnp.sum(got[1:].astype(jnp.float32), axis=0)
        if stage != "x":
            acc = acc.reshape(RING, -1, width)
    return (row_loss, head_grad, acc.astype(jnp.bfloat16))


def solution(mesh):
    tok_n = mesh.shape["tok"]
    voc_n = mesh.shape["voc"]
    placed = (P(("tok", "voc"), None), P(("tok", "voc"), None), P(), P())

    def body(h, w, ti, tl):
        return per_device(h, w, ti, tl, tok_n, voc_n)

    return jax.shard_map(
        body,
        mesh=mesh,
        in_specs=placed,
        out_specs=(P(("tok", "voc")), P(("tok", "voc"), None), P(("tok", "voc"), None)),
        check_vma=False,
    )
```

```python
import jax
import jax.numpy as jnp
from jax import lax
from jax.sharding import PartitionSpec as P

loss_scale = 256.0
RING = 4


HITS = 8


def dense_target(local, probs, voc_dev):
    blocks = local.shape[0] // 64
    local_b = local.reshape(blocks, 64, local.shape[1])
    probs_b = probs.reshape(blocks, 64, probs.shape[1])
    columns = jnp.arange(voc_dev, dtype=jnp.int32)[None, None, :]

    def one_block(args):
        block_local, block_probs = args
        equal = block_local[:, :, None] == columns
        return jnp.sum(jnp.where(equal, block_probs[:, :, None], 0.0), axis=1)

    return lax.map(one_block, (local_b, probs_b)).reshape(local.shape[0], voc_dev)


def compact_target(local, probs, voc_dev):
    valid = (local >= 0) & (local < voc_dev)
    rank = jnp.cumsum(valid.astype(jnp.int32), axis=1) - 1
    slot = jnp.arange(HITS, dtype=jnp.int32)[None, None, :]
    chosen = valid[:, :, None] & (rank[:, :, None] == slot)
    slot_local = jnp.sum(jnp.where(chosen, local[:, :, None], 0), axis=1)
    slot_probs = jnp.sum(jnp.where(chosen, probs[:, :, None], 0.0), axis=1)
    columns = jnp.arange(voc_dev, dtype=jnp.int32)[None, :]
    target = jnp.zeros((local.shape[0], voc_dev), jnp.float32)
    for j in range(HITS):
        target = target + jnp.where(slot_local[:, j : j + 1] == columns, slot_probs[:, j : j + 1], 0.0)
    return target


def teacher_target(local, probs, voc_dev):
    valid = (local >= 0) & (local < voc_dev)
    crowded = jnp.any(jnp.sum(valid.astype(jnp.int32), axis=1) > HITS)
    return lax.cond(
        crowded,
        lambda: dense_target(local, probs, voc_dev),
        lambda: compact_target(local, probs, voc_dev),
    )


def coords():
    tok = lax.axis_index("tok")
    voc = lax.axis_index("voc")
    return {"x": tok // RING, "y": tok % RING, "z": voc // 2, "c": voc % 2}


def stage_pairs(stage, shift, tok_n, voc_n):
    if stage == "c":
        return "voc", [(v, v ^ 1) for v in range(voc_n)]
    if stage == "z":
        return "voc", [(v, ((v // 2 + shift) % RING) * 2 + v % 2) for v in range(voc_n)]
    if stage == "y":
        return "tok", [(t, (t // RING) * RING + (t % RING + shift) % RING) for t in range(tok_n)]
    return "tok", [(t, ((t // RING + shift) % RING) * RING + t % RING) for t in range(tok_n)]


def exchange(block_for, stage, tok_n, voc_n):
    n = 2 if stage == "c" else RING
    got = [block_for(0)]
    for shift in range(1, n):
        axis, pairs = stage_pairs(stage, shift, tok_n, voc_n)
        got.append(lax.ppermute(block_for(shift), axis, pairs))
    return jnp.stack(got)


def arrival_tokens(at):
    r = jnp.arange(2 * RING ** 3 * 4, dtype=jnp.int32)
    i = r % 4
    x = (at["x"] - (r // 4) % RING) % RING
    y = (at["y"] - (r // 16) % RING) % RING
    z = (at["z"] - (r // 64) % RING) % RING
    c = at["c"] ^ (r // 256)
    return (((x * RING + y) * RING + z) * 2 + c) * 4 + i


def natural_rows(at):
    t = jnp.arange(2 * RING ** 3 * 4, dtype=jnp.int32)
    i = t % 4
    s_c = at["c"] ^ ((t // 4) % 2)
    s_z = (at["z"] - (t // 8) % RING) % RING
    s_y = (at["y"] - (t // 32) % RING) % RING
    s_x = (at["x"] - (t // 128) % RING) % RING
    return (((s_c * RING + s_z) * RING + s_y) * RING + s_x) * 4 + i


def per_device(hidden_rows, head_weight, teacher_index, teacher_logprob, tok_n, voc_n):
    voc_dev = head_weight.shape[0]
    tok_dev = hidden_rows.shape[0]
    width = hidden_rows.shape[1]
    at = coords()

    position = lax.axis_index(("tok", "voc"))
    offset = position * voc_dev
    rows = arrival_tokens(at)
    index_arr = jnp.take(teacher_index, rows, axis=0)
    logprob_arr = jnp.take(teacher_logprob, rows, axis=0)
    local = index_arr - offset
    probs_arr = jnp.exp(logprob_arr)
    target = teacher_target(local, probs_arr, voc_dev)

    every = hidden_rows
    for stage in ("x", "y", "z", "c"):
        got = exchange(lambda s: every, stage, tok_n, voc_n)
        every = got.reshape(-1, width)
        if stage == "z":
            every, target = lax.optimization_barrier((every, target))

    logits = lax.dot_general(
        every, head_weight, (((1,), (1,)), ((), ())), preferred_element_type=jnp.float32
    )
    part_dot = jnp.sum(logits * target, axis=1)
    local_peak = jnp.max(logits, axis=1)
    local_sum = jnp.sum(jnp.exp(logits - local_peak[:, None]), axis=1)

    stats = jnp.take(jnp.stack([local_peak, local_sum, part_dot]), natural_rows(at), axis=1)
    for stage in ("c", "z", "y", "x"):
        got = exchange(lambda s: stats, stage, tok_n, voc_n)
        peak = jnp.max(got[:, 0], axis=0)
        summed = jnp.sum(got[:, 1] * jnp.exp(got[:, 0] - peak[None]), axis=0)
        dotted = jnp.sum(got[:, 2], axis=0)
        stats = jnp.stack([peak, summed, dotted])
    peak, summed, dotted = stats[0], stats[1], stats[2]

    lse = peak + jnp.log(summed)
    probs = jnp.exp(teacher_logprob)
    total_p = jnp.sum(probs, axis=1)
    own_term = jnp.sum(probs * teacher_logprob, axis=1)
    loss_all = own_term - dotted + total_p * lse
    row_loss = lax.dynamic_slice_in_dim(loss_all, position * tok_dev, tok_dev, 0)
    lse_arr = jnp.take(lse, rows, axis=0)
    total_arr = jnp.sum(probs_arr, axis=1)
    grad = (loss_scale * (total_arr[:, None] * jnp.exp(logits - lse_arr[:, None]) - target)).astype(
        jnp.bfloat16
    )
    partial = jnp.dot(grad, head_weight, preferred_element_type=jnp.float32)
    head_grad = lax.dot_general(
        grad, every, (((0,), (0,)), ((), ())), preferred_element_type=jnp.float32
    ).astype(jnp.bfloat16)

    acc = partial.reshape(2, -1, width)
    for stage in ("c", "z", "y", "x"):
        n = acc.shape[0]
        got = exchange(lambda s: acc[(-s) % n].astype(jnp.bfloat16), stage, tok_n, voc_n)
        acc = acc[0] + jnp.sum(got[1:].astype(jnp.float32), axis=0)
        if stage == "z":
            acc, head_grad = lax.optimization_barrier((acc, head_grad))
        if stage != "x":
            acc = acc.reshape(RING, -1, width)
    return (row_loss, head_grad, acc.astype(jnp.bfloat16))


def solution(mesh):
    tok_n = mesh.shape["tok"]
    voc_n = mesh.shape["voc"]
    placed = (P(("tok", "voc"), None), P(("tok", "voc"), None), P(), P())

    def body(h, w, ti, tl):
        return per_device(h, w, ti, tl, tok_n, voc_n)

    return jax.shard_map(
        body,
        mesh=mesh,
        in_specs=placed,
        out_specs=(P(("tok", "voc")), P(("tok", "voc"), None), P(("tok", "voc"), None)),
        check_vma=False,
    )
```

```python
import jax
import jax.numpy as jnp
from jax import lax
from jax.sharding import PartitionSpec as P

loss_scale = 256.0
RING = 4


HITS = 8


def dense_target(local, probs, voc_dev):
    blocks = local.shape[0] // 64
    local_b = local.reshape(blocks, 64, local.shape[1])
    probs_b = probs.reshape(blocks, 64, probs.shape[1])
    columns = jnp.arange(voc_dev, dtype=jnp.int32)[None, None, :]

    def one_block(args):
        block_local, block_probs = args
        equal = block_local[:, :, None] == columns
        return jnp.sum(jnp.where(equal, block_probs[:, :, None], 0.0), axis=1)

    return lax.map(one_block, (local_b, probs_b)).reshape(local.shape[0], voc_dev)


def compact_target(local, probs, voc_dev):
    valid = (local >= 0) & (local < voc_dev)
    rank = jnp.cumsum(valid.astype(jnp.int32), axis=1) - 1
    slot = jnp.arange(HITS, dtype=jnp.int32)[None, None, :]
    chosen = valid[:, :, None] & (rank[:, :, None] == slot)
    slot_local = jnp.sum(jnp.where(chosen, local[:, :, None], 0), axis=1)
    slot_probs = jnp.sum(jnp.where(chosen, probs[:, :, None], 0.0), axis=1)
    columns = jnp.arange(voc_dev, dtype=jnp.int32)[None, :]
    target = jnp.zeros((local.shape[0], voc_dev), jnp.float32)
    for j in range(HITS):
        target = target + jnp.where(slot_local[:, j : j + 1] == columns, slot_probs[:, j : j + 1], 0.0)
    return target


def teacher_target(local, probs, voc_dev):
    valid = (local >= 0) & (local < voc_dev)
    crowded = jnp.any(jnp.sum(valid.astype(jnp.int32), axis=1) > HITS)
    return lax.cond(
        crowded,
        lambda: dense_target(local, probs, voc_dev),
        lambda: compact_target(local, probs, voc_dev),
    )


def coords():
    tok = lax.axis_index("tok")
    voc = lax.axis_index("voc")
    return {"x": tok // RING, "y": tok % RING, "z": voc // 2, "c": voc % 2}


AXES = ("tok", "voc")


def device_coords(d, voc_n):
    tok, voc = divmod(d, voc_n)
    return tok // RING, tok % RING, voc // 2, voc % 2


def device_id(x, y, z, c, voc_n):
    return (x * RING + y) * voc_n + z * 2 + c


def ring_axis(stage, core):
    if stage == "r1":
        return "x" if core == 0 else "z"
    if stage == "r3":
        return "z" if core == 0 else "x"
    if stage == "r2":
        return "y"
    return stage


def stage_pairs(stage, shift, n_dev, voc_n):
    pairs = []
    for d in range(n_dev):
        x, y, z, c = device_coords(d, voc_n)
        axis = ring_axis(stage, c)
        if axis == "c":
            c = c ^ 1
        elif axis == "x":
            x = (x + shift) % RING
        elif axis == "y":
            y = (y + shift) % RING
        else:
            z = (z + shift) % RING
        pairs.append((d, device_id(x, y, z, c, voc_n)))
    return pairs


def exchange(block_for, stage, n_dev, voc_n):
    n = 2 if stage == "c" else RING
    got = [block_for(0)]
    for shift in range(1, n):
        got.append(lax.ppermute(block_for(shift), AXES, stage_pairs(stage, shift, n_dev, voc_n)))
    return jnp.stack(got)


def arrival_tokens(at):
    r = jnp.arange(2 * RING ** 3 * 4, dtype=jnp.int32)
    i = r % 4
    s_r1 = (r // 4) % RING
    s_r2 = (r // 16) % RING
    s_r3 = (r // 64) % RING
    c = at["c"] ^ (r // 256)
    s_x = jnp.where(c == 0, s_r1, s_r3)
    s_z = jnp.where(c == 0, s_r3, s_r1)
    x = (at["x"] - s_x) % RING
    y = (at["y"] - s_r2) % RING
    z = (at["z"] - s_z) % RING
    return (((x * RING + y) * RING + z) * 2 + c) * 4 + i


def natural_rows(at):
    t = jnp.arange(2 * RING ** 3 * 4, dtype=jnp.int32)
    i = t % 4
    c = (t // 4) % 2
    s_c = at["c"] ^ c
    s_z = (at["z"] - (t // 8) % RING) % RING
    s_y = (at["y"] - (t // 32) % RING) % RING
    s_x = (at["x"] - (t // 128) % RING) % RING
    s_r1 = jnp.where(c == 0, s_x, s_z)
    s_r3 = jnp.where(c == 0, s_z, s_x)
    return (((s_c * RING + s_r3) * RING + s_y) * RING + s_r1) * 4 + i


def per_device(hidden_rows, head_weight, teacher_index, teacher_logprob, n_dev, voc_n):
    voc_dev = head_weight.shape[0]
    tok_dev = hidden_rows.shape[0]
    width = hidden_rows.shape[1]
    at = coords()

    position = lax.axis_index(("tok", "voc"))
    offset = position * voc_dev
    rows = arrival_tokens(at)
    index_arr = jnp.take(teacher_index, rows, axis=0)
    logprob_arr = jnp.take(teacher_logprob, rows, axis=0)
    local = index_arr - offset
    probs_arr = jnp.exp(logprob_arr)
    target = teacher_target(local, probs_arr, voc_dev)

    every = hidden_rows
    for stage in ("r1", "r2", "r3", "c"):
        got = exchange(lambda s: every, stage, n_dev, voc_n)
        every = got.reshape(-1, width)
        if stage == "r3":
            every, target = lax.optimization_barrier((every, target))

    logits = lax.dot_general(
        every, head_weight, (((1,), (1,)), ((), ())), preferred_element_type=jnp.float32
    )
    part_dot = jnp.sum(logits * target, axis=1)
    local_peak = jnp.max(logits, axis=1)
    local_sum = jnp.sum(jnp.exp(logits - local_peak[:, None]), axis=1)

    stats = jnp.take(jnp.stack([local_peak, local_sum, part_dot]), natural_rows(at), axis=1)
    for stage in ("c", "z", "y", "x"):
        got = exchange(lambda s: stats, stage, n_dev, voc_n)
        peak = jnp.max(got[:, 0], axis=0)
        summed = jnp.sum(got[:, 1] * jnp.exp(got[:, 0] - peak[None]), axis=0)
        dotted = jnp.sum(got[:, 2], axis=0)
        stats = jnp.stack([peak, summed, dotted])
    peak, summed, dotted = stats[0], stats[1], stats[2]

    lse = peak + jnp.log(summed)
    probs = jnp.exp(teacher_logprob)
    total_p = jnp.sum(probs, axis=1)
    own_term = jnp.sum(probs * teacher_logprob, axis=1)
    loss_all = own_term - dotted + total_p * lse
    row_loss = lax.dynamic_slice_in_dim(loss_all, position * tok_dev, tok_dev, 0)
    lse_arr = jnp.take(lse, rows, axis=0)
    total_arr = jnp.sum(probs_arr, axis=1)
    grad = (loss_scale * (total_arr[:, None] * jnp.exp(logits - lse_arr[:, None]) - target)).astype(
        jnp.bfloat16
    )
    partial = jnp.dot(grad, head_weight, preferred_element_type=jnp.float32)
    head_grad = lax.dot_general(
        grad, every, (((0,), (0,)), ((), ())), preferred_element_type=jnp.float32
    ).astype(jnp.bfloat16)

    acc = partial.reshape(2, -1, width)
    for stage in ("c", "r3", "r2", "r1"):
        n = acc.shape[0]
        got = exchange(lambda s: acc[(-s) % n].astype(jnp.bfloat16), stage, n_dev, voc_n)
        acc = acc[0] + jnp.sum(got[1:].astype(jnp.float32), axis=0)
        if stage == "r3":
            acc, head_grad = lax.optimization_barrier((acc, head_grad))
        if stage != "r1":
            acc = acc.reshape(RING, -1, width)
    return (row_loss, head_grad, acc.astype(jnp.bfloat16))


def solution(mesh):
    voc_n = mesh.shape["voc"]
    n_dev = mesh.shape["tok"] * voc_n
    placed = (P(("tok", "voc"), None), P(("tok", "voc"), None), P(), P())

    def body(h, w, ti, tl):
        return per_device(h, w, ti, tl, n_dev, voc_n)

    return jax.shard_map(
        body,
        mesh=mesh,
        in_specs=placed,
        out_specs=(P(("tok", "voc")), P(("tok", "voc"), None), P(("tok", "voc"), None)),
        check_vma=False,
    )
```

```python
import jax
import jax.numpy as jnp
from jax import lax
from jax.sharding import PartitionSpec as P

loss_scale = 256.0
RING = 4


HITS = 8


def dense_target(local, probs, voc_dev):
    blocks = local.shape[0] // 64
    local_b = local.reshape(blocks, 64, local.shape[1])
    probs_b = probs.reshape(blocks, 64, probs.shape[1])
    columns = jnp.arange(voc_dev, dtype=jnp.int32)[None, None, :]

    def one_block(args):
        block_local, block_probs = args
        equal = block_local[:, :, None] == columns
        return jnp.sum(jnp.where(equal, block_probs[:, :, None], 0.0), axis=1)

    return lax.map(one_block, (local_b, probs_b)).reshape(local.shape[0], voc_dev)


def compact_target(local, probs, voc_dev):
    valid = (local >= 0) & (local < voc_dev)
    rank = jnp.cumsum(valid.astype(jnp.int32), axis=1) - 1
    slot = jnp.arange(HITS, dtype=jnp.int32)[None, None, :]
    chosen = valid[:, :, None] & (rank[:, :, None] == slot)
    slot_local = jnp.sum(jnp.where(chosen, local[:, :, None], 0), axis=1)
    slot_probs = jnp.sum(jnp.where(chosen, probs[:, :, None], 0.0), axis=1)
    columns = jnp.arange(voc_dev, dtype=jnp.int32)[None, :]
    target = jnp.zeros((local.shape[0], voc_dev), jnp.float32)
    for j in range(HITS):
        target = target + jnp.where(slot_local[:, j : j + 1] == columns, slot_probs[:, j : j + 1], 0.0)
    return target


def teacher_target(local, probs, voc_dev):
    valid = (local >= 0) & (local < voc_dev)
    crowded = jnp.any(jnp.sum(valid.astype(jnp.int32), axis=1) > HITS)
    return lax.cond(
        crowded,
        lambda: dense_target(local, probs, voc_dev),
        lambda: compact_target(local, probs, voc_dev),
    )


def coords():
    tok = lax.axis_index("tok")
    voc = lax.axis_index("voc")
    return {"x": tok // RING, "y": tok % RING, "z": voc // 2, "c": voc % 2}


AXES = ("tok", "voc")


def device_coords(d, voc_n):
    tok, voc = divmod(d, voc_n)
    return tok // RING, tok % RING, voc // 2, voc % 2


def device_id(x, y, z, c, voc_n):
    return (x * RING + y) * voc_n + z * 2 + c


def ring_axis(stage, core):
    if stage == "r1":
        return "x" if core == 0 else "z"
    if stage == "r3":
        return "z" if core == 0 else "x"
    if stage == "r2":
        return "y"
    return stage


def stage_pairs(stage, shift, n_dev, voc_n):
    pairs = []
    for d in range(n_dev):
        x, y, z, c = device_coords(d, voc_n)
        axis = ring_axis(stage, c)
        if axis == "c":
            c = c ^ 1
        elif axis == "x":
            x = (x + shift) % RING
        elif axis == "y":
            y = (y + shift) % RING
        else:
            z = (z + shift) % RING
        pairs.append((d, device_id(x, y, z, c, voc_n)))
    return pairs


def exchange(block_for, stage, n_dev, voc_n):
    n = 2 if stage == "c" else RING
    got = [block_for(0)]
    for shift in range(1, n):
        got.append(lax.ppermute(block_for(shift), AXES, stage_pairs(stage, shift, n_dev, voc_n)))
    return jnp.stack(got)


def arrival_tokens(at):
    r = jnp.arange(2 * RING ** 3 * 4, dtype=jnp.int32)
    i = r % 4
    s_r1 = (r // 4) % RING
    s_r2 = (r // 16) % RING
    s_r3 = (r // 64) % RING
    c = at["c"] ^ (r // 256)
    s_x = jnp.where(c == 0, s_r1, s_r3)
    s_z = jnp.where(c == 0, s_r3, s_r1)
    x = (at["x"] - s_x) % RING
    y = (at["y"] - s_r2) % RING
    z = (at["z"] - s_z) % RING
    return (((x * RING + y) * RING + z) * 2 + c) * 4 + i


def natural_rows(at):
    t = jnp.arange(2 * RING ** 3 * 4, dtype=jnp.int32)
    i = t % 4
    c = (t // 4) % 2
    s_c = at["c"] ^ c
    s_z = (at["z"] - (t // 8) % RING) % RING
    s_y = (at["y"] - (t // 32) % RING) % RING
    s_x = (at["x"] - (t // 128) % RING) % RING
    s_r1 = jnp.where(c == 0, s_x, s_z)
    s_r3 = jnp.where(c == 0, s_z, s_x)
    return (((s_c * RING + s_r3) * RING + s_y) * RING + s_r1) * 4 + i


def half_logits(rows_block, head_weight):
    return lax.dot_general(
        rows_block, head_weight, (((1,), (1,)), ((), ())), preferred_element_type=jnp.float32
    )


def per_device(hidden_rows, head_weight, teacher_index, teacher_logprob, n_dev, voc_n):
    voc_dev = head_weight.shape[0]
    tok_dev = hidden_rows.shape[0]
    width = hidden_rows.shape[1]
    at = coords()

    position = lax.axis_index(("tok", "voc"))
    offset = position * voc_dev
    rows = arrival_tokens(at)
    index_arr = jnp.take(teacher_index, rows, axis=0)
    logprob_arr = jnp.take(teacher_logprob, rows, axis=0)
    local = index_arr - offset
    probs_arr = jnp.exp(logprob_arr)
    target = teacher_target(local, probs_arr, voc_dev)

    own = hidden_rows
    for stage in ("r1", "r2", "r3"):
        own = exchange(lambda s: own, stage, n_dev, voc_n).reshape(-1, width)
        if stage == "r3":
            own, target = lax.optimization_barrier((own, target))
    other = lax.ppermute(own, AXES, stage_pairs("c", 1, n_dev, voc_n))
    logits_own = half_logits(own, head_weight)
    logits_other = half_logits(other, head_weight)
    every = jnp.concatenate([own, other], axis=0)
    half = own.shape[0]
    target_own, target_other = target[:half], target[half:]

    def local_stats(logits, tgt):
        peak = jnp.max(logits, axis=1)
        return peak, jnp.sum(jnp.exp(logits - peak[:, None]), axis=1), jnp.sum(logits * tgt, axis=1)

    own_stats = local_stats(logits_own, target_own)
    other_stats = local_stats(logits_other, target_other)
    stats = jnp.stack([jnp.concatenate([a, b]) for a, b in zip(own_stats, other_stats)])

    stats = jnp.take(stats, natural_rows(at), axis=1)
    for stage in ("c", "z", "y", "x"):
        got = exchange(lambda s: stats, stage, n_dev, voc_n)
        peak = jnp.max(got[:, 0], axis=0)
        summed = jnp.sum(got[:, 1] * jnp.exp(got[:, 0] - peak[None]), axis=0)
        dotted = jnp.sum(got[:, 2], axis=0)
        stats = jnp.stack([peak, summed, dotted])
    peak, summed, dotted = stats[0], stats[1], stats[2]

    lse = peak + jnp.log(summed)
    probs = jnp.exp(teacher_logprob)
    total_p = jnp.sum(probs, axis=1)
    own_term = jnp.sum(probs * teacher_logprob, axis=1)
    loss_all = own_term - dotted + total_p * lse
    row_loss = lax.dynamic_slice_in_dim(loss_all, position * tok_dev, tok_dev, 0)
    back = jnp.take(jnp.stack([lse, total_p], axis=1), rows, axis=0)
    lse_arr, total_arr = back[:, 0], back[:, 1]

    def half_grad(logits, tgt, lse_h, total_h):
        return (loss_scale * (total_h[:, None] * jnp.exp(logits - lse_h[:, None]) - tgt)).astype(
            jnp.bfloat16
        )

    grad_other = half_grad(logits_other, target_other, lse_arr[half:], total_arr[half:])
    grad_own = half_grad(logits_own, target_own, lse_arr[:half], total_arr[:half])

    sent = jnp.dot(grad_other, head_weight, preferred_element_type=jnp.float32).astype(jnp.bfloat16)
    received = lax.ppermute(sent, AXES, stage_pairs("c", 1, n_dev, voc_n))
    acc = jnp.dot(grad_own, head_weight, preferred_element_type=jnp.float32)
    acc, received = lax.optimization_barrier((acc, received))
    acc = (acc + received.astype(jnp.float32)).reshape(RING, -1, width)
    grad = jnp.concatenate([grad_own, grad_other], axis=0)
    head_grad = lax.dot_general(
        grad, every, (((0,), (0,)), ((), ())), preferred_element_type=jnp.float32
    ).astype(jnp.bfloat16)
    for stage in ("r3", "r2", "r1"):
        got = exchange(lambda s: acc[(-s) % RING].astype(jnp.bfloat16), stage, n_dev, voc_n)
        acc = acc[0] + jnp.sum(got[1:].astype(jnp.float32), axis=0)
        if stage == "r3":
            acc, head_grad = lax.optimization_barrier((acc, head_grad))
        if stage != "r1":
            acc = acc.reshape(RING, -1, width)
    return (row_loss, head_grad, acc.astype(jnp.bfloat16))


def solution(mesh):
    voc_n = mesh.shape["voc"]
    n_dev = mesh.shape["tok"] * voc_n
    placed = (P(("tok", "voc"), None), P(("tok", "voc"), None), P(), P())

    def body(h, w, ti, tl):
        return per_device(h, w, ti, tl, n_dev, voc_n)

    return jax.shard_map(
        body,
        mesh=mesh,
        in_specs=placed,
        out_specs=(P(("tok", "voc")), P(("tok", "voc"), None), P(("tok", "voc"), None)),
        check_vma=False,
    )
```

```python
import jax
import jax.numpy as jnp
from jax import lax
from jax.sharding import PartitionSpec as P
from jax.experimental import pallas as pl
from jax.experimental.pallas import tpu as pltpu

loss_scale = 256.0
RING = 4


HITS = 8


def dense_target(local, probs, voc_dev):
    blocks = local.shape[0] // 64
    local_b = local.reshape(blocks, 64, local.shape[1])
    probs_b = probs.reshape(blocks, 64, probs.shape[1])
    columns = jnp.arange(voc_dev, dtype=jnp.int32)[None, None, :]

    def one_block(args):
        block_local, block_probs = args
        equal = block_local[:, :, None] == columns
        return jnp.sum(jnp.where(equal, block_probs[:, :, None], 0.0), axis=1)

    return lax.map(one_block, (local_b, probs_b)).reshape(local.shape[0], voc_dev)


def compact_target(local, probs, voc_dev):
    valid = (local >= 0) & (local < voc_dev)
    rank = jnp.cumsum(valid.astype(jnp.int32), axis=1) - 1
    slot = jnp.arange(HITS, dtype=jnp.int32)[None, None, :]
    chosen = valid[:, :, None] & (rank[:, :, None] == slot)
    slot_local = jnp.sum(jnp.where(chosen, local[:, :, None], 0), axis=1)
    slot_probs = jnp.sum(jnp.where(chosen, probs[:, :, None], 0.0), axis=1)
    columns = jnp.arange(voc_dev, dtype=jnp.int32)[None, :]
    target = jnp.zeros((local.shape[0], voc_dev), jnp.float32)
    for j in range(HITS):
        target = target + jnp.where(slot_local[:, j : j + 1] == columns, slot_probs[:, j : j + 1], 0.0)
    return target


def teacher_target(local, probs, voc_dev):
    valid = (local >= 0) & (local < voc_dev)
    crowded = jnp.any(jnp.sum(valid.astype(jnp.int32), axis=1) > HITS)
    return lax.cond(
        crowded,
        lambda: dense_target(local, probs, voc_dev),
        lambda: compact_target(local, probs, voc_dev),
    )


def coords():
    tok = lax.axis_index("tok")
    voc = lax.axis_index("voc")
    return {"x": tok // RING, "y": tok % RING, "z": voc // 2, "c": voc % 2}


AXES = ("tok", "voc")


def device_coords(d, voc_n):
    tok, voc = divmod(d, voc_n)
    return tok // RING, tok % RING, voc // 2, voc % 2


def device_id(x, y, z, c, voc_n):
    return (x * RING + y) * voc_n + z * 2 + c


def ring_axis(stage, core):
    if stage == "r1":
        return "x" if core == 0 else "z"
    if stage == "r3":
        return "z" if core == 0 else "x"
    if stage == "r2":
        return "y"
    return stage


def stage_pairs(stage, shift, n_dev, voc_n):
    pairs = []
    for d in range(n_dev):
        x, y, z, c = device_coords(d, voc_n)
        axis = ring_axis(stage, c)
        if axis == "c":
            c = c ^ 1
        elif axis == "x":
            x = (x + shift) % RING
        elif axis == "y":
            y = (y + shift) % RING
        else:
            z = (z + shift) % RING
        pairs.append((d, device_id(x, y, z, c, voc_n)))
    return pairs


def exchange(block_for, stage, n_dev, voc_n):
    n = 2 if stage == "c" else RING
    got = [block_for(0)]
    for shift in range(1, n):
        got.append(lax.ppermute(block_for(shift), AXES, stage_pairs(stage, shift, n_dev, voc_n)))
    return jnp.stack(got)


def arrival_tokens(at):
    r = jnp.arange(2 * RING ** 3 * 4, dtype=jnp.int32)
    i = r % 4
    s_r1 = (r // 4) % RING
    s_r2 = (r // 16) % RING
    s_r3 = (r // 64) % RING
    c = at["c"] ^ (r // 256)
    s_x = jnp.where(c == 0, s_r1, s_r3)
    s_z = jnp.where(c == 0, s_r3, s_r1)
    x = (at["x"] - s_x) % RING
    y = (at["y"] - s_r2) % RING
    z = (at["z"] - s_z) % RING
    return (((x * RING + y) * RING + z) * 2 + c) * 4 + i


def natural_rows(at):
    t = jnp.arange(2 * RING ** 3 * 4, dtype=jnp.int32)
    i = t % 4
    c = (t // 4) % 2
    s_c = at["c"] ^ c
    s_z = (at["z"] - (t // 8) % RING) % RING
    s_y = (at["y"] - (t // 32) % RING) % RING
    s_x = (at["x"] - (t // 128) % RING) % RING
    s_r1 = jnp.where(c == 0, s_x, s_z)
    s_r3 = jnp.where(c == 0, s_z, s_x)
    return (((s_c * RING + s_r3) * RING + s_y) * RING + s_r1) * 4 + i


def _rows_by_weight(g_ref, w_ref, o_ref):
    o_ref[...] = jnp.dot(g_ref[...], w_ref[...], preferred_element_type=jnp.float32).astype(o_ref.dtype)


def rows_by_weight(g, w, out_dtype, tile=512):
    m, k = g.shape
    n = w.shape[1]
    return pl.pallas_call(
        _rows_by_weight,
        grid=(n // tile,),
        in_specs=[pl.BlockSpec((m, k), lambda j: (0, 0)), pl.BlockSpec((k, tile), lambda j: (0, j))],
        out_specs=pl.BlockSpec((m, tile), lambda j: (0, j)),
        out_shape=jax.ShapeDtypeStruct((m, n), out_dtype),
        cost_estimate=pl.CostEstimate(
            flops=2 * m * k * n,
            transcendentals=0,
            bytes_accessed=(m * k + k * n) * 2 + m * n * jnp.dtype(out_dtype).itemsize,
        ),
    )(g, w)


def _rows_by_weight_t(x_ref, w_ref, o_ref):
    o_ref[...] = lax.dot_general(
        x_ref[...], w_ref[...], (((1,), (1,)), ((), ())), preferred_element_type=jnp.float32
    )


def half_logits(x, w, tile=384):
    m, d = x.shape
    v = w.shape[0]
    return pl.pallas_call(
        _rows_by_weight_t,
        grid=(v // tile,),
        in_specs=[pl.BlockSpec((m, d), lambda j: (0, 0)), pl.BlockSpec((tile, d), lambda j: (j, 0))],
        out_specs=pl.BlockSpec((m, tile), lambda j: (0, j)),
        out_shape=jax.ShapeDtypeStruct((m, v), jnp.float32),
        cost_estimate=pl.CostEstimate(
            flops=2 * m * d * v, transcendentals=0, bytes_accessed=(m * d + v * d) * 2 + m * v * 4
        ),
    )(x, w)


def per_device(hidden_rows, head_weight, teacher_index, teacher_logprob, n_dev, voc_n):
    voc_dev = head_weight.shape[0]
    tok_dev = hidden_rows.shape[0]
    width = hidden_rows.shape[1]
    at = coords()

    position = lax.axis_index(("tok", "voc"))
    offset = position * voc_dev
    rows = arrival_tokens(at)
    index_arr = jnp.take(teacher_index, rows, axis=0)
    logprob_arr = jnp.take(teacher_logprob, rows, axis=0)
    local = index_arr - offset
    probs_arr = jnp.exp(logprob_arr)
    target = teacher_target(local, probs_arr, voc_dev)

    own = hidden_rows
    for stage in ("r1", "r2", "r3"):
        own = exchange(lambda s: own, stage, n_dev, voc_n).reshape(-1, width)
        if stage == "r3":
            own, target = lax.optimization_barrier((own, target))
    other = lax.ppermute(own, AXES, stage_pairs("c", 1, n_dev, voc_n))
    logits_own = half_logits(own, head_weight)
    logits_other = half_logits(other, head_weight)
    every = jnp.concatenate([own, other], axis=0)
    half = own.shape[0]
    target_own, target_other = target[:half], target[half:]

    def local_stats(logits, tgt):
        peak = jnp.max(logits, axis=1)
        return peak, jnp.sum(jnp.exp(logits - peak[:, None]), axis=1), jnp.sum(logits * tgt, axis=1)

    own_stats = local_stats(logits_own, target_own)
    other_stats = local_stats(logits_other, target_other)
    stats = jnp.stack([jnp.concatenate([a, b]) for a, b in zip(own_stats, other_stats)])

    stats = jnp.take(stats, natural_rows(at), axis=1)
    for stage in ("c", "z", "y", "x"):
        got = exchange(lambda s: stats, stage, n_dev, voc_n)
        peak = jnp.max(got[:, 0], axis=0)
        summed = jnp.sum(got[:, 1] * jnp.exp(got[:, 0] - peak[None]), axis=0)
        dotted = jnp.sum(got[:, 2], axis=0)
        stats = jnp.stack([peak, summed, dotted])
    peak, summed, dotted = stats[0], stats[1], stats[2]

    lse = peak + jnp.log(summed)
    probs = jnp.exp(teacher_logprob)
    total_p = jnp.sum(probs, axis=1)
    own_term = jnp.sum(probs * teacher_logprob, axis=1)
    loss_all = own_term - dotted + total_p * lse
    row_loss = lax.dynamic_slice_in_dim(loss_all, position * tok_dev, tok_dev, 0)
    back = jnp.take(jnp.stack([lse, total_p], axis=1), rows, axis=0)
    lse_arr, total_arr = back[:, 0], back[:, 1]

    def half_grad(logits, tgt, lse_h, total_h):
        return (loss_scale * (total_h[:, None] * jnp.exp(logits - lse_h[:, None]) - tgt)).astype(
            jnp.bfloat16
        )

    grad_other = half_grad(logits_other, target_other, lse_arr[half:], total_arr[half:])
    grad_own = half_grad(logits_own, target_own, lse_arr[:half], total_arr[:half])

    sent = rows_by_weight(grad_other, head_weight, jnp.bfloat16)
    received = lax.ppermute(sent, AXES, stage_pairs("c", 1, n_dev, voc_n))
    acc = rows_by_weight(grad_own, head_weight, jnp.float32)
    acc, received = lax.optimization_barrier((acc, received))
    acc = (acc + received.astype(jnp.float32)).reshape(RING, -1, width)
    grad = jnp.concatenate([grad_own, grad_other], axis=0)
    head_grad = lax.dot_general(
        grad, every, (((0,), (0,)), ((), ())), preferred_element_type=jnp.float32
    ).astype(jnp.bfloat16)
    for stage in ("r3", "r2", "r1"):
        got = exchange(lambda s: acc[(-s) % RING].astype(jnp.bfloat16), stage, n_dev, voc_n)
        acc = acc[0] + jnp.sum(got[1:].astype(jnp.float32), axis=0)
        if stage == "r3":
            acc, head_grad = lax.optimization_barrier((acc, head_grad))
        if stage != "r1":
            acc = acc.reshape(RING, -1, width)
    return (row_loss, head_grad, acc.astype(jnp.bfloat16))


def solution(mesh):
    voc_n = mesh.shape["voc"]
    n_dev = mesh.shape["tok"] * voc_n
    placed = (P(("tok", "voc"), None), P(("tok", "voc"), None), P(), P())

    def body(h, w, ti, tl):
        return per_device(h, w, ti, tl, n_dev, voc_n)

    return jax.shard_map(
        body,
        mesh=mesh,
        in_specs=placed,
        out_specs=(P(("tok", "voc")), P(("tok", "voc"), None), P(("tok", "voc"), None)),
        check_vma=False,
    )
```

```python
import jax
import jax.numpy as jnp
from jax import lax
from jax.sharding import PartitionSpec as P

loss_scale = 256.0
RING = 4


HITS = 8


def dense_target(local, probs, voc_dev):
    blocks = local.shape[0] // 64
    local_b = local.reshape(blocks, 64, local.shape[1])
    probs_b = probs.reshape(blocks, 64, probs.shape[1])
    columns = jnp.arange(voc_dev, dtype=jnp.int32)[None, None, :]

    def one_block(args):
        block_local, block_probs = args
        equal = block_local[:, :, None] == columns
        return jnp.sum(jnp.where(equal, block_probs[:, :, None], 0.0), axis=1)

    return lax.map(one_block, (local_b, probs_b)).reshape(local.shape[0], voc_dev)


def compact_target(local, probs, voc_dev):
    valid = (local >= 0) & (local < voc_dev)
    rank = jnp.cumsum(valid.astype(jnp.int32), axis=1) - 1
    slot = jnp.arange(HITS, dtype=jnp.int32)[None, None, :]
    chosen = valid[:, :, None] & (rank[:, :, None] == slot)
    slot_local = jnp.sum(jnp.where(chosen, local[:, :, None], 0), axis=1)
    slot_probs = jnp.sum(jnp.where(chosen, probs[:, :, None], 0.0), axis=1)
    columns = jnp.arange(voc_dev, dtype=jnp.int32)[None, :]
    target = jnp.zeros((local.shape[0], voc_dev), jnp.float32)
    for j in range(HITS):
        target = target + jnp.where(slot_local[:, j : j + 1] == columns, slot_probs[:, j : j + 1], 0.0)
    return target


def teacher_target(local, probs, voc_dev):
    valid = (local >= 0) & (local < voc_dev)
    crowded = jnp.any(jnp.sum(valid.astype(jnp.int32), axis=1) > HITS)
    return lax.cond(
        crowded,
        lambda: dense_target(local, probs, voc_dev),
        lambda: compact_target(local, probs, voc_dev),
    )


def coords():
    tok = lax.axis_index("tok")
    voc = lax.axis_index("voc")
    return {"x": tok // RING, "y": tok % RING, "z": voc // 2, "c": voc % 2}


AXES = ("tok", "voc")


def device_coords(d, voc_n):
    tok, voc = divmod(d, voc_n)
    return tok // RING, tok % RING, voc // 2, voc % 2


def device_id(x, y, z, c, voc_n):
    return (x * RING + y) * voc_n + z * 2 + c


def ring_axis(stage, core):
    if stage == "r1":
        return "x" if core == 0 else "z"
    if stage == "r3":
        return "z" if core == 0 else "x"
    if stage == "r2":
        return "y"
    return stage


def stage_pairs(stage, shift, n_dev, voc_n):
    pairs = []
    for d in range(n_dev):
        x, y, z, c = device_coords(d, voc_n)
        axis = ring_axis(stage, c)
        if axis == "c":
            c = c ^ 1
        elif axis == "x":
            x = (x + shift) % RING
        elif axis == "y":
            y = (y + shift) % RING
        else:
            z = (z + shift) % RING
        pairs.append((d, device_id(x, y, z, c, voc_n)))
    return pairs


def exchange(block_for, stage, n_dev, voc_n):
    n = 2 if stage == "c" else RING
    got = [block_for(0)]
    for shift in range(1, n):
        got.append(lax.ppermute(block_for(shift), AXES, stage_pairs(stage, shift, n_dev, voc_n)))
    return jnp.stack(got)


def arrival_tokens(at):
    r = jnp.arange(2 * RING ** 3 * 4, dtype=jnp.int32)
    i = r % 4
    s_r1 = (r // 4) % RING
    s_r2 = (r // 16) % RING
    s_r3 = (r // 64) % RING
    c = at["c"] ^ (r // 256)
    s_x = jnp.where(c == 0, s_r1, s_r3)
    s_z = jnp.where(c == 0, s_r3, s_r1)
    x = (at["x"] - s_x) % RING
    y = (at["y"] - s_r2) % RING
    z = (at["z"] - s_z) % RING
    return (((x * RING + y) * RING + z) * 2 + c) * 4 + i


def natural_rows(at):
    t = jnp.arange(2 * RING ** 3 * 4, dtype=jnp.int32)
    i = t % 4
    c = (t // 4) % 2
    s_c = at["c"] ^ c
    s_z = (at["z"] - (t // 8) % RING) % RING
    s_y = (at["y"] - (t // 32) % RING) % RING
    s_x = (at["x"] - (t // 128) % RING) % RING
    s_r1 = jnp.where(c == 0, s_x, s_z)
    s_r3 = jnp.where(c == 0, s_z, s_x)
    return (((s_c * RING + s_r3) * RING + s_y) * RING + s_r1) * 4 + i


def half_logits(rows_block, head_weight):
    return lax.dot_general(
        rows_block, head_weight, (((1,), (1,)), ((), ())), preferred_element_type=jnp.float32
    )


def per_device(hidden_rows, head_weight, teacher_index, teacher_logprob, n_dev, voc_n):
    voc_dev = head_weight.shape[0]
    tok_dev = hidden_rows.shape[0]
    width = hidden_rows.shape[1]
    at = coords()

    position = lax.axis_index(("tok", "voc"))
    offset = position * voc_dev
    rows = arrival_tokens(at)
    index_arr = jnp.take(teacher_index, rows, axis=0)
    logprob_arr = jnp.take(teacher_logprob, rows, axis=0)
    local = index_arr - offset
    probs_arr = jnp.exp(logprob_arr)
    target = teacher_target(local, probs_arr, voc_dev)

    own = hidden_rows
    for stage in ("r1", "r2", "r3"):
        own = exchange(lambda s: own, stage, n_dev, voc_n).reshape(-1, width)
        if stage == "r3":
            own, target = lax.optimization_barrier((own, target))
    other = lax.ppermute(own, AXES, stage_pairs("c", 1, n_dev, voc_n))
    logits_own = half_logits(own, head_weight)
    logits_other = half_logits(other, head_weight)
    every = jnp.concatenate([own, other], axis=0)
    half = own.shape[0]
    target_own, target_other = target[:half], target[half:]

    def local_stats(logits, tgt):
        peak = jnp.max(logits, axis=1)
        return peak, jnp.sum(jnp.exp(logits - peak[:, None]), axis=1), jnp.sum(logits * tgt, axis=1)

    own_stats = local_stats(logits_own, target_own)
    other_stats = local_stats(logits_other, target_other)
    stats = jnp.stack([jnp.concatenate([a, b]) for a, b in zip(own_stats, other_stats)])

    stats = jnp.take(stats, natural_rows(at), axis=1)
    for stage in ("c", "z", "y", "x"):
        got = exchange(lambda s: stats, stage, n_dev, voc_n)
        peak = jnp.max(got[:, 0], axis=0)
        summed = jnp.sum(got[:, 1] * jnp.exp(got[:, 0] - peak[None]), axis=0)
        dotted = jnp.sum(got[:, 2], axis=0)
        stats = jnp.stack([peak, summed, dotted])
    peak, summed, dotted = stats[0], stats[1], stats[2]

    lse = peak + jnp.log(summed)
    probs = jnp.exp(teacher_logprob)
    total_p = jnp.sum(probs, axis=1)
    own_term = jnp.sum(probs * teacher_logprob, axis=1)
    loss_all = own_term - dotted + total_p * lse
    row_loss = lax.dynamic_slice_in_dim(loss_all, position * tok_dev, tok_dev, 0)
    back = jnp.take(jnp.stack([lse, total_p], axis=1), rows, axis=0)
    lse_arr, total_arr = back[:, 0], back[:, 1]

    def half_grad(logits, tgt, lse_h, total_h):
        return (loss_scale * (total_h[:, None] * jnp.exp(logits - lse_h[:, None]) - tgt)).astype(
            jnp.bfloat16
        )

    grad_other = half_grad(logits_other, target_other, lse_arr[half:], total_arr[half:])

    sent = jnp.dot(grad_other, head_weight, preferred_element_type=jnp.float32).astype(jnp.bfloat16)
    received = lax.ppermute(sent, AXES, stage_pairs("c", 1, n_dev, voc_n))
    sent, logits_own = lax.optimization_barrier((sent, logits_own))
    grad_own = half_grad(logits_own, target_own, lse_arr[:half], total_arr[:half])
    acc = jnp.dot(grad_own, head_weight, preferred_element_type=jnp.float32)
    acc, received = lax.optimization_barrier((acc, received))
    acc = (acc + received.astype(jnp.float32)).reshape(RING, -1, width)
    grad = jnp.concatenate([grad_own, grad_other], axis=0)
    head_grad = lax.dot_general(
        grad, every, (((0,), (0,)), ((), ())), preferred_element_type=jnp.float32
    ).astype(jnp.bfloat16)
    for stage in ("r3", "r2", "r1"):
        got = exchange(lambda s: acc[(-s) % RING].astype(jnp.bfloat16), stage, n_dev, voc_n)
        acc = acc[0] + jnp.sum(got[1:].astype(jnp.float32), axis=0)
        if stage == "r3":
            acc, head_grad = lax.optimization_barrier((acc, head_grad))
        if stage != "r1":
            acc = acc.reshape(RING, -1, width)
    return (row_loss, head_grad, acc.astype(jnp.bfloat16))


def solution(mesh):
    voc_n = mesh.shape["voc"]
    n_dev = mesh.shape["tok"] * voc_n
    placed = (P(("tok", "voc"), None), P(("tok", "voc"), None), P(), P())

    def body(h, w, ti, tl):
        return per_device(h, w, ti, tl, n_dev, voc_n)

    return jax.shard_map(
        body,
        mesh=mesh,
        in_specs=placed,
        out_specs=(P(("tok", "voc")), P(("tok", "voc"), None), P(("tok", "voc"), None)),
        check_vma=False,
    )
```

```python
import jax
import jax.numpy as jnp
from jax import lax
from jax.sharding import PartitionSpec as P

loss_scale = 256.0
RING = 4


HITS = 8


def dense_target(local, probs, voc_dev):
    blocks = local.shape[0] // 64
    local_b = local.reshape(blocks, 64, local.shape[1])
    probs_b = probs.reshape(blocks, 64, probs.shape[1])
    columns = jnp.arange(voc_dev, dtype=jnp.int32)[None, None, :]

    def one_block(args):
        block_local, block_probs = args
        equal = block_local[:, :, None] == columns
        return jnp.sum(jnp.where(equal, block_probs[:, :, None], 0.0), axis=1)

    return lax.map(one_block, (local_b, probs_b)).reshape(local.shape[0], voc_dev)


def compact_target(local, probs, voc_dev):
    valid = (local >= 0) & (local < voc_dev)
    rank = jnp.cumsum(valid.astype(jnp.int32), axis=1) - 1
    slot = jnp.arange(HITS, dtype=jnp.int32)[None, None, :]
    chosen = valid[:, :, None] & (rank[:, :, None] == slot)
    slot_local = jnp.sum(jnp.where(chosen, local[:, :, None], 0), axis=1)
    slot_probs = jnp.sum(jnp.where(chosen, probs[:, :, None], 0.0), axis=1)
    columns = jnp.arange(voc_dev, dtype=jnp.int32)[None, :]
    target = jnp.zeros((local.shape[0], voc_dev), jnp.float32)
    for j in range(HITS):
        target = target + jnp.where(slot_local[:, j : j + 1] == columns, slot_probs[:, j : j + 1], 0.0)
    return target


def teacher_target(local, probs, voc_dev):
    valid = (local >= 0) & (local < voc_dev)
    crowded = jnp.any(jnp.sum(valid.astype(jnp.int32), axis=1) > HITS)
    return lax.cond(
        crowded,
        lambda: dense_target(local, probs, voc_dev),
        lambda: compact_target(local, probs, voc_dev),
    )


def coords():
    tok = lax.axis_index("tok")
    voc = lax.axis_index("voc")
    return {"x": tok // RING, "y": tok % RING, "z": voc // 2, "c": voc % 2}


AXES = ("tok", "voc")


def device_coords(d, voc_n):
    tok, voc = divmod(d, voc_n)
    return tok // RING, tok % RING, voc // 2, voc % 2


def device_id(x, y, z, c, voc_n):
    return (x * RING + y) * voc_n + z * 2 + c


def ring_axis(stage, core):
    if stage == "r1":
        return "x" if core == 0 else "z"
    if stage == "r3":
        return "z" if core == 0 else "x"
    if stage == "r2":
        return "y"
    return stage


def stage_pairs(stage, shift, n_dev, voc_n):
    pairs = []
    for d in range(n_dev):
        x, y, z, c = device_coords(d, voc_n)
        axis = ring_axis(stage, c)
        if axis == "c":
            c = c ^ 1
        elif axis == "x":
            x = (x + shift) % RING
        elif axis == "y":
            y = (y + shift) % RING
        else:
            z = (z + shift) % RING
        pairs.append((d, device_id(x, y, z, c, voc_n)))
    return pairs


def exchange(block_for, stage, n_dev, voc_n):
    n = 2 if stage == "c" else RING
    got = [block_for(0)]
    for shift in range(1, n):
        got.append(lax.ppermute(block_for(shift), AXES, stage_pairs(stage, shift, n_dev, voc_n)))
    return jnp.stack(got)


def arrival_tokens(at):
    r = jnp.arange(2 * RING ** 3 * 4, dtype=jnp.int32)
    i = r % 4
    s_r1 = (r // 4) % RING
    s_r2 = (r // 16) % RING
    s_r3 = (r // 64) % RING
    c = at["c"] ^ (r // 256)
    s_x = jnp.where(c == 0, s_r1, s_r3)
    s_z = jnp.where(c == 0, s_r3, s_r1)
    x = (at["x"] - s_x) % RING
    y = (at["y"] - s_r2) % RING
    z = (at["z"] - s_z) % RING
    return (((x * RING + y) * RING + z) * 2 + c) * 4 + i


def natural_rows(at):
    t = jnp.arange(2 * RING ** 3 * 4, dtype=jnp.int32)
    i = t % 4
    c = (t // 4) % 2
    s_c = at["c"] ^ c
    s_z = (at["z"] - (t // 8) % RING) % RING
    s_y = (at["y"] - (t // 32) % RING) % RING
    s_x = (at["x"] - (t // 128) % RING) % RING
    s_r1 = jnp.where(c == 0, s_x, s_z)
    s_r3 = jnp.where(c == 0, s_z, s_x)
    return (((s_c * RING + s_r3) * RING + s_y) * RING + s_r1) * 4 + i


def half_logits(rows_block, head_weight):
    return lax.dot_general(
        rows_block, head_weight, (((1,), (1,)), ((), ())), preferred_element_type=jnp.float32
    )


def per_device(hidden_rows, head_weight, teacher_index, teacher_logprob, n_dev, voc_n):
    voc_dev = head_weight.shape[0]
    tok_dev = hidden_rows.shape[0]
    width = hidden_rows.shape[1]
    at = coords()

    position = lax.axis_index(("tok", "voc"))
    offset = position * voc_dev
    rows = arrival_tokens(at)
    index_arr = jnp.take(teacher_index, rows, axis=0)
    logprob_arr = jnp.take(teacher_logprob, rows, axis=0)
    local = index_arr - offset
    probs_arr = jnp.exp(logprob_arr)
    target = teacher_target(local, probs_arr, voc_dev)

    own = hidden_rows
    for stage in ("r1", "r2"):
        own = exchange(lambda s: own, stage, n_dev, voc_n).reshape(-1, width)
    got = exchange(lambda s: own, "r3", n_dev, voc_n)
    first_logits = half_logits(own, head_weight)
    got, target, first_logits = lax.optimization_barrier((got, target, first_logits))
    own = got.reshape(-1, width)
    other = lax.ppermute(own, AXES, stage_pairs("c", 1, n_dev, voc_n))
    logits_own = jnp.concatenate(
        [first_logits, half_logits(got[1:].reshape(-1, width), head_weight)], axis=0
    )
    logits_other = half_logits(other, head_weight)
    every = jnp.concatenate([own, other], axis=0)
    half = own.shape[0]
    target_own, target_other = target[:half], target[half:]

    def local_stats(logits, tgt):
        peak = jnp.max(logits, axis=1)
        return peak, jnp.sum(jnp.exp(logits - peak[:, None]), axis=1), jnp.sum(logits * tgt, axis=1)

    own_stats = local_stats(logits_own, target_own)
    other_stats = local_stats(logits_other, target_other)
    stats = jnp.stack([jnp.concatenate([a, b]) for a, b in zip(own_stats, other_stats)])

    stats = jnp.take(stats, natural_rows(at), axis=1)
    for stage in ("c", "z", "y", "x"):
        got = exchange(lambda s: stats, stage, n_dev, voc_n)
        peak = jnp.max(got[:, 0], axis=0)
        summed = jnp.sum(got[:, 1] * jnp.exp(got[:, 0] - peak[None]), axis=0)
        dotted = jnp.sum(got[:, 2], axis=0)
        stats = jnp.stack([peak, summed, dotted])
    peak, summed, dotted = stats[0], stats[1], stats[2]

    lse = peak + jnp.log(summed)
    probs = jnp.exp(teacher_logprob)
    total_p = jnp.sum(probs, axis=1)
    own_term = jnp.sum(probs * teacher_logprob, axis=1)
    loss_all = own_term - dotted + total_p * lse
    row_loss = lax.dynamic_slice_in_dim(loss_all, position * tok_dev, tok_dev, 0)
    back = jnp.take(jnp.stack([lse, total_p], axis=1), rows, axis=0)
    lse_arr, total_arr = back[:, 0], back[:, 1]

    def half_grad(logits, tgt, lse_h, total_h):
        return (loss_scale * (total_h[:, None] * jnp.exp(logits - lse_h[:, None]) - tgt)).astype(
            jnp.bfloat16
        )

    grad_other = half_grad(logits_other, target_other, lse_arr[half:], total_arr[half:])

    sent = jnp.dot(grad_other, head_weight, preferred_element_type=jnp.float32).astype(jnp.bfloat16)
    received = lax.ppermute(sent, AXES, stage_pairs("c", 1, n_dev, voc_n))
    sent, logits_own = lax.optimization_barrier((sent, logits_own))
    grad_own = half_grad(logits_own, target_own, lse_arr[:half], total_arr[:half])
    acc = jnp.dot(grad_own, head_weight, preferred_element_type=jnp.float32)
    acc, received = lax.optimization_barrier((acc, received))
    acc = (acc + received.astype(jnp.float32)).reshape(RING, -1, width)
    grad = jnp.concatenate([grad_own, grad_other], axis=0)
    head_grad = lax.dot_general(
        grad, every, (((0,), (0,)), ((), ())), preferred_element_type=jnp.float32
    ).astype(jnp.bfloat16)
    for stage in ("r3", "r2", "r1"):
        got = exchange(lambda s: acc[(-s) % RING].astype(jnp.bfloat16), stage, n_dev, voc_n)
        acc = acc[0] + jnp.sum(got[1:].astype(jnp.float32), axis=0)
        if stage == "r3":
            acc, head_grad = lax.optimization_barrier((acc, head_grad))
        if stage != "r1":
            acc = acc.reshape(RING, -1, width)
    return (row_loss, head_grad, acc.astype(jnp.bfloat16))


def solution(mesh):
    voc_n = mesh.shape["voc"]
    n_dev = mesh.shape["tok"] * voc_n
    placed = (P(("tok", "voc"), None), P(("tok", "voc"), None), P(), P())

    def body(h, w, ti, tl):
        return per_device(h, w, ti, tl, n_dev, voc_n)

    return jax.shard_map(
        body,
        mesh=mesh,
        in_specs=placed,
        out_specs=(P(("tok", "voc")), P(("tok", "voc"), None), P(("tok", "voc"), None)),
        check_vma=False,
    )
```

```python
import jax
import jax.numpy as jnp
from jax import lax
from jax.sharding import PartitionSpec as P

loss_scale = 256.0
RING = 4


HITS = 8


def dense_target(local, probs, voc_dev):
    blocks = local.shape[0] // 64
    local_b = local.reshape(blocks, 64, local.shape[1])
    probs_b = probs.reshape(blocks, 64, probs.shape[1])
    columns = jnp.arange(voc_dev, dtype=jnp.int32)[None, None, :]

    def one_block(args):
        block_local, block_probs = args
        equal = block_local[:, :, None] == columns
        return jnp.sum(jnp.where(equal, block_probs[:, :, None], 0.0), axis=1)

    return lax.map(one_block, (local_b, probs_b)).reshape(local.shape[0], voc_dev)


def compact_target(local, probs, voc_dev):
    valid = (local >= 0) & (local < voc_dev)
    rank = jnp.cumsum(valid.astype(jnp.int32), axis=1) - 1
    slot = jnp.arange(HITS, dtype=jnp.int32)[None, None, :]
    chosen = valid[:, :, None] & (rank[:, :, None] == slot)
    slot_local = jnp.sum(jnp.where(chosen, local[:, :, None], 0), axis=1)
    slot_probs = jnp.sum(jnp.where(chosen, probs[:, :, None], 0.0), axis=1)
    columns = jnp.arange(voc_dev, dtype=jnp.int32)[None, :]
    target = jnp.zeros((local.shape[0], voc_dev), jnp.float32)
    for j in range(HITS):
        target = target + jnp.where(slot_local[:, j : j + 1] == columns, slot_probs[:, j : j + 1], 0.0)
    return target


def teacher_target(local, probs, voc_dev):
    valid = (local >= 0) & (local < voc_dev)
    crowded = jnp.any(jnp.sum(valid.astype(jnp.int32), axis=1) > HITS)
    return lax.cond(
        crowded,
        lambda: dense_target(local, probs, voc_dev),
        lambda: compact_target(local, probs, voc_dev),
    )


def coords():
    tok = lax.axis_index("tok")
    voc = lax.axis_index("voc")
    return {"x": tok // RING, "y": tok % RING, "z": voc // 2, "c": voc % 2}


AXES = ("tok", "voc")


def device_coords(d, voc_n):
    tok, voc = divmod(d, voc_n)
    return tok // RING, tok % RING, voc // 2, voc % 2


def device_id(x, y, z, c, voc_n):
    return (x * RING + y) * voc_n + z * 2 + c


def ring_axis(stage, core):
    if stage == "r1":
        return "x" if core == 0 else "z"
    if stage == "r3":
        return "z" if core == 0 else "x"
    if stage == "r2":
        return "y"
    return stage


def stage_pairs(stage, shift, n_dev, voc_n):
    pairs = []
    for d in range(n_dev):
        x, y, z, c = device_coords(d, voc_n)
        axis = ring_axis(stage, c)
        if axis == "c":
            c = c ^ 1
        elif axis == "x":
            x = (x + shift) % RING
        elif axis == "y":
            y = (y + shift) % RING
        else:
            z = (z + shift) % RING
        pairs.append((d, device_id(x, y, z, c, voc_n)))
    return pairs


def exchange(block_for, stage, n_dev, voc_n):
    n = 2 if stage == "c" else RING
    got = [block_for(0)]
    for shift in range(1, n):
        got.append(lax.ppermute(block_for(shift), AXES, stage_pairs(stage, shift, n_dev, voc_n)))
    return jnp.stack(got)


def arrival_tokens(at):
    r = jnp.arange(2 * RING ** 3 * 4, dtype=jnp.int32)
    i = r % 4
    s_r1 = (r // 4) % RING
    s_r2 = (r // 16) % RING
    s_r3 = (r // 64) % RING
    c = at["c"] ^ (r // 256)
    s_x = jnp.where(c == 0, s_r1, s_r3)
    s_z = jnp.where(c == 0, s_r3, s_r1)
    x = (at["x"] - s_x) % RING
    y = (at["y"] - s_r2) % RING
    z = (at["z"] - s_z) % RING
    return (((x * RING + y) * RING + z) * 2 + c) * 4 + i


def natural_rows(at):
    t = jnp.arange(2 * RING ** 3 * 4, dtype=jnp.int32)
    i = t % 4
    c = (t // 4) % 2
    s_c = at["c"] ^ c
    s_z = (at["z"] - (t // 8) % RING) % RING
    s_y = (at["y"] - (t // 32) % RING) % RING
    s_x = (at["x"] - (t // 128) % RING) % RING
    s_r1 = jnp.where(c == 0, s_x, s_z)
    s_r3 = jnp.where(c == 0, s_z, s_x)
    return (((s_c * RING + s_r3) * RING + s_y) * RING + s_r1) * 4 + i


def half_logits(rows_block, head_weight):
    return lax.dot_general(
        rows_block, head_weight, (((1,), (1,)), ((), ())), preferred_element_type=jnp.float32
    )


def per_device(hidden_rows, head_weight, teacher_index, teacher_logprob, n_dev, voc_n):
    voc_dev = head_weight.shape[0]
    tok_dev = hidden_rows.shape[0]
    width = hidden_rows.shape[1]
    at = coords()

    position = lax.axis_index(("tok", "voc"))
    offset = position * voc_dev
    rows = arrival_tokens(at)
    index_arr = jnp.take(teacher_index, rows, axis=0)
    logprob_arr = jnp.take(teacher_logprob, rows, axis=0)
    local = index_arr - offset
    probs_arr = jnp.exp(logprob_arr)
    target = teacher_target(local, probs_arr, voc_dev)

    own = hidden_rows
    for stage in ("r1", "r2", "r3"):
        own = exchange(lambda s: own, stage, n_dev, voc_n).reshape(-1, width)
        if stage == "r3":
            own, target = lax.optimization_barrier((own, target))
    other = lax.ppermute(own, AXES, stage_pairs("c", 1, n_dev, voc_n))
    logits_own = half_logits(own, head_weight)
    logits_other = half_logits(other, head_weight)
    every = jnp.concatenate([own, other], axis=0)
    half = own.shape[0]
    target_own, target_other = target[:half], target[half:]

    def local_stats(logits, tgt):
        peak = jnp.max(logits, axis=1)
        return peak, jnp.sum(jnp.exp(logits - peak[:, None]), axis=1), jnp.sum(logits * tgt, axis=1)

    own_stats = local_stats(logits_own, target_own)
    other_stats = local_stats(logits_other, target_other)
    stats = jnp.stack([jnp.concatenate([a, b]) for a, b in zip(own_stats, other_stats)])

    place = (rows[:, None] == jnp.arange(rows.shape[0], dtype=jnp.int32)[None, :]).astype(jnp.float32)
    stats = jnp.dot(stats, place, precision=lax.Precision.HIGHEST)
    for stage in ("c", "z", "y", "x"):
        got = exchange(lambda s: stats, stage, n_dev, voc_n)
        peak = jnp.max(got[:, 0], axis=0)
        summed = jnp.sum(got[:, 1] * jnp.exp(got[:, 0] - peak[None]), axis=0)
        dotted = jnp.sum(got[:, 2], axis=0)
        stats = jnp.stack([peak, summed, dotted])
    peak, summed, dotted = stats[0], stats[1], stats[2]

    lse = peak + jnp.log(summed)
    probs = jnp.exp(teacher_logprob)
    total_p = jnp.sum(probs, axis=1)
    own_term = jnp.sum(probs * teacher_logprob, axis=1)
    loss_all = own_term - dotted + total_p * lse
    row_loss = lax.dynamic_slice_in_dim(loss_all, position * tok_dev, tok_dev, 0)
    back = jnp.dot(place, jnp.stack([lse, total_p], axis=1), precision=lax.Precision.HIGHEST)
    lse_arr, total_arr = back[:, 0], back[:, 1]

    def half_grad(logits, tgt, lse_h, total_h):
        return (loss_scale * (total_h[:, None] * jnp.exp(logits - lse_h[:, None]) - tgt)).astype(
            jnp.bfloat16
        )

    grad_other = half_grad(logits_other, target_other, lse_arr[half:], total_arr[half:])

    sent = jnp.dot(grad_other, head_weight, preferred_element_type=jnp.float32).astype(jnp.bfloat16)
    received = lax.ppermute(sent, AXES, stage_pairs("c", 1, n_dev, voc_n))
    sent, logits_own = lax.optimization_barrier((sent, logits_own))
    grad_own = half_grad(logits_own, target_own, lse_arr[:half], total_arr[:half])
    acc = jnp.dot(grad_own, head_weight, preferred_element_type=jnp.float32)
    acc, received = lax.optimization_barrier((acc, received))
    acc = (acc + received.astype(jnp.float32)).reshape(RING, -1, width)
    grad = jnp.concatenate([grad_own, grad_other], axis=0)
    head_grad = lax.dot_general(
        grad, every, (((0,), (0,)), ((), ())), preferred_element_type=jnp.float32
    ).astype(jnp.bfloat16)
    for stage in ("r3", "r2", "r1"):
        got = exchange(lambda s: acc[(-s) % RING].astype(jnp.bfloat16), stage, n_dev, voc_n)
        acc = acc[0] + jnp.sum(got[1:].astype(jnp.float32), axis=0)
        if stage == "r3":
            acc, head_grad = lax.optimization_barrier((acc, head_grad))
        if stage != "r1":
            acc = acc.reshape(RING, -1, width)
    return (row_loss, head_grad, acc.astype(jnp.bfloat16))


def solution(mesh):
    voc_n = mesh.shape["voc"]
    n_dev = mesh.shape["tok"] * voc_n
    placed = (P(("tok", "voc"), None), P(("tok", "voc"), None), P(), P())

    def body(h, w, ti, tl):
        return per_device(h, w, ti, tl, n_dev, voc_n)

    return jax.shard_map(
        body,
        mesh=mesh,
        in_specs=placed,
        out_specs=(P(("tok", "voc")), P(("tok", "voc"), None), P(("tok", "voc"), None)),
        check_vma=False,
    )
```

```python
import jax
import jax.numpy as jnp
from jax import lax
from jax.sharding import PartitionSpec as P

loss_scale = 256.0
RING = 4


HITS = 8


def dense_target(local, probs, voc_dev):
    blocks = local.shape[0] // 64
    local_b = local.reshape(blocks, 64, local.shape[1])
    probs_b = probs.reshape(blocks, 64, probs.shape[1])
    columns = jnp.arange(voc_dev, dtype=jnp.int32)[None, None, :]

    def one_block(args):
        block_local, block_probs = args
        equal = block_local[:, :, None] == columns
        return jnp.sum(jnp.where(equal, block_probs[:, :, None], 0.0), axis=1)

    return lax.map(one_block, (local_b, probs_b)).reshape(local.shape[0], voc_dev)


def compact_target(local, probs, voc_dev):
    valid = (local >= 0) & (local < voc_dev)
    rank = jnp.cumsum(valid.astype(jnp.int32), axis=1) - 1
    slot = jnp.arange(HITS, dtype=jnp.int32)[None, None, :]
    chosen = valid[:, :, None] & (rank[:, :, None] == slot)
    slot_local = jnp.sum(jnp.where(chosen, local[:, :, None], 0), axis=1)
    slot_probs = jnp.sum(jnp.where(chosen, probs[:, :, None], 0.0), axis=1)
    columns = jnp.arange(voc_dev, dtype=jnp.int32)[None, :]
    target = jnp.zeros((local.shape[0], voc_dev), jnp.float32)
    for j in range(HITS):
        target = target + jnp.where(slot_local[:, j : j + 1] == columns, slot_probs[:, j : j + 1], 0.0)
    return target


def teacher_target(local, probs, voc_dev):
    valid = (local >= 0) & (local < voc_dev)
    crowded = jnp.any(jnp.sum(valid.astype(jnp.int32), axis=1) > HITS)
    return lax.cond(
        crowded,
        lambda: dense_target(local, probs, voc_dev),
        lambda: compact_target(local, probs, voc_dev),
    )


def coords():
    tok = lax.axis_index("tok")
    voc = lax.axis_index("voc")
    return {"x": tok // RING, "y": tok % RING, "z": voc // 2, "c": voc % 2}


AXES = ("tok", "voc")


def device_coords(d, voc_n):
    tok, voc = divmod(d, voc_n)
    return tok // RING, tok % RING, voc // 2, voc % 2


def device_id(x, y, z, c, voc_n):
    return (x * RING + y) * voc_n + z * 2 + c


def ring_axis(stage, core):
    if stage == "r1":
        return "y"
    if stage == "r2":
        return "x" if core == 0 else "z"
    if stage == "r3":
        return "z" if core == 0 else "x"
    return stage


def stage_pairs(stage, shift, n_dev, voc_n):
    pairs = []
    for d in range(n_dev):
        x, y, z, c = device_coords(d, voc_n)
        axis = ring_axis(stage, c)
        if axis == "c":
            c = c ^ 1
        elif axis == "x":
            x = (x + shift) % RING
        elif axis == "y":
            y = (y + shift) % RING
        else:
            z = (z + shift) % RING
        pairs.append((d, device_id(x, y, z, c, voc_n)))
    return pairs


def exchange(block_for, stage, n_dev, voc_n):
    n = 2 if stage == "c" else RING
    got = [block_for(0)]
    for shift in range(1, n):
        got.append(lax.ppermute(block_for(shift), AXES, stage_pairs(stage, shift, n_dev, voc_n)))
    return jnp.stack(got)


def arrival_tokens(at):
    r = jnp.arange(2 * RING ** 3 * 4, dtype=jnp.int32)
    i = r % 4
    s_r1 = (r // 4) % RING
    s_r2 = (r // 16) % RING
    s_r3 = (r // 64) % RING
    c = at["c"] ^ (r // 256)
    s_x = jnp.where(c == 0, s_r2, s_r3)
    s_z = jnp.where(c == 0, s_r3, s_r2)
    x = (at["x"] - s_x) % RING
    y = (at["y"] - s_r1) % RING
    z = (at["z"] - s_z) % RING
    return (((x * RING + y) * RING + z) * 2 + c) * 4 + i


def natural_rows(at):
    t = jnp.arange(2 * RING ** 3 * 4, dtype=jnp.int32)
    i = t % 4
    c = (t // 4) % 2
    s_c = at["c"] ^ c
    s_z = (at["z"] - (t // 8) % RING) % RING
    s_y = (at["y"] - (t // 32) % RING) % RING
    s_x = (at["x"] - (t // 128) % RING) % RING
    s_r2 = jnp.where(c == 0, s_x, s_z)
    s_r3 = jnp.where(c == 0, s_z, s_x)
    return (((s_c * RING + s_r3) * RING + s_r2) * RING + s_y) * 4 + i


def half_logits(rows_block, head_weight):
    return lax.dot_general(
        rows_block, head_weight, (((1,), (1,)), ((), ())), preferred_element_type=jnp.float32
    )


def per_device(hidden_rows, head_weight, teacher_index, teacher_logprob, n_dev, voc_n):
    voc_dev = head_weight.shape[0]
    tok_dev = hidden_rows.shape[0]
    width = hidden_rows.shape[1]
    at = coords()

    position = lax.axis_index(("tok", "voc"))
    offset = position * voc_dev
    rows = arrival_tokens(at)
    index_arr = jnp.take(teacher_index, rows, axis=0)
    logprob_arr = jnp.take(teacher_logprob, rows, axis=0)
    local = index_arr - offset
    probs_arr = jnp.exp(logprob_arr)
    target = teacher_target(local, probs_arr, voc_dev)

    own = hidden_rows
    for stage in ("r1", "r2", "r3"):
        own = exchange(lambda s: own, stage, n_dev, voc_n).reshape(-1, width)
        if stage == "r3":
            own, target = lax.optimization_barrier((own, target))
    other = lax.ppermute(own, AXES, stage_pairs("c", 1, n_dev, voc_n))
    logits_own = half_logits(own, head_weight)
    logits_other = half_logits(other, head_weight)
    every = jnp.concatenate([own, other], axis=0)
    half = own.shape[0]
    target_own, target_other = target[:half], target[half:]

    def local_stats(logits, tgt):
        peak = jnp.max(logits, axis=1)
        return peak, jnp.sum(jnp.exp(logits - peak[:, None]), axis=1), jnp.sum(logits * tgt, axis=1)

    own_stats = local_stats(logits_own, target_own)
    other_stats = local_stats(logits_other, target_other)
    stats = jnp.stack([jnp.concatenate([a, b]) for a, b in zip(own_stats, other_stats)])

    place = (rows[:, None] == jnp.arange(rows.shape[0], dtype=jnp.int32)[None, :]).astype(jnp.float32)
    stats = jnp.dot(stats, place, precision=lax.Precision.HIGHEST)
    for stage in ("c", "z", "y", "x"):
        got = exchange(lambda s: stats, stage, n_dev, voc_n)
        peak = jnp.max(got[:, 0], axis=0)
        summed = jnp.sum(got[:, 1] * jnp.exp(got[:, 0] - peak[None]), axis=0)
        dotted = jnp.sum(got[:, 2], axis=0)
        stats = jnp.stack([peak, summed, dotted])
    peak, summed, dotted = stats[0], stats[1], stats[2]

    lse = peak + jnp.log(summed)
    probs = jnp.exp(teacher_logprob)
    total_p = jnp.sum(probs, axis=1)
    own_term = jnp.sum(probs * teacher_logprob, axis=1)
    loss_all = own_term - dotted + total_p * lse
    row_loss = lax.dynamic_slice_in_dim(loss_all, position * tok_dev, tok_dev, 0)
    back = jnp.dot(place, jnp.stack([lse, total_p], axis=1), precision=lax.Precision.HIGHEST)
    lse_arr, total_arr = back[:, 0], back[:, 1]

    def half_grad(logits, tgt, lse_h, total_h):
        return (loss_scale * (total_h[:, None] * jnp.exp(logits - lse_h[:, None]) - tgt)).astype(
            jnp.bfloat16
        )

    grad_other = half_grad(logits_other, target_other, lse_arr[half:], total_arr[half:])

    sent = jnp.dot(grad_other, head_weight, preferred_element_type=jnp.float32).astype(jnp.bfloat16)
    received = lax.ppermute(sent, AXES, stage_pairs("c", 1, n_dev, voc_n))
    sent, logits_own = lax.optimization_barrier((sent, logits_own))
    grad_own = half_grad(logits_own, target_own, lse_arr[:half], total_arr[:half])
    acc = jnp.dot(grad_own, head_weight, preferred_element_type=jnp.float32)
    acc, received = lax.optimization_barrier((acc, received))
    acc = (acc + received.astype(jnp.float32)).reshape(RING, -1, width)
    grad = jnp.concatenate([grad_own, grad_other], axis=0)
    head_grad = lax.dot_general(
        grad, every, (((0,), (0,)), ((), ())), preferred_element_type=jnp.float32
    ).astype(jnp.bfloat16)
    for stage in ("r3", "r2", "r1"):
        got = exchange(lambda s: acc[(-s) % RING].astype(jnp.bfloat16), stage, n_dev, voc_n)
        acc = acc[0] + jnp.sum(got[1:].astype(jnp.float32), axis=0)
        if stage == "r3":
            acc, head_grad = lax.optimization_barrier((acc, head_grad))
        if stage != "r1":
            acc = acc.reshape(RING, -1, width)
    return (row_loss, head_grad, acc.astype(jnp.bfloat16))


def solution(mesh):
    voc_n = mesh.shape["voc"]
    n_dev = mesh.shape["tok"] * voc_n
    placed = (P(("tok", "voc"), None), P(("tok", "voc"), None), P(), P())

    def body(h, w, ti, tl):
        return per_device(h, w, ti, tl, n_dev, voc_n)

    return jax.shard_map(
        body,
        mesh=mesh,
        in_specs=placed,
        out_specs=(P(("tok", "voc")), P(("tok", "voc"), None), P(("tok", "voc"), None)),
        check_vma=False,
    )
```

```python
import jax
import jax.numpy as jnp
from jax import lax
from jax.sharding import PartitionSpec as P

loss_scale = 256.0
RING = 4


HITS = 8


def dense_target(local, probs, voc_dev):
    blocks = local.shape[0] // 64
    local_b = local.reshape(blocks, 64, local.shape[1])
    probs_b = probs.reshape(blocks, 64, probs.shape[1])
    columns = jnp.arange(voc_dev, dtype=jnp.int32)[None, None, :]

    def one_block(args):
        block_local, block_probs = args
        equal = block_local[:, :, None] == columns
        return jnp.sum(jnp.where(equal, block_probs[:, :, None], 0.0), axis=1)

    return lax.map(one_block, (local_b, probs_b)).reshape(local.shape[0], voc_dev)


def compact_target(local, probs, voc_dev):
    valid = (local >= 0) & (local < voc_dev)
    rank = jnp.cumsum(valid.astype(jnp.int32), axis=1) - 1
    slot = jnp.arange(HITS, dtype=jnp.int32)[None, None, :]
    chosen = valid[:, :, None] & (rank[:, :, None] == slot)
    slot_local = jnp.sum(jnp.where(chosen, local[:, :, None], 0), axis=1)
    slot_probs = jnp.sum(jnp.where(chosen, probs[:, :, None], 0.0), axis=1)
    columns = jnp.arange(voc_dev, dtype=jnp.int32)[None, :]
    target = jnp.zeros((local.shape[0], voc_dev), jnp.float32)
    for j in range(HITS):
        target = target + jnp.where(slot_local[:, j : j + 1] == columns, slot_probs[:, j : j + 1], 0.0)
    return target


def teacher_target(local, probs, voc_dev):
    valid = (local >= 0) & (local < voc_dev)
    crowded = jnp.any(jnp.sum(valid.astype(jnp.int32), axis=1) > HITS)
    return lax.cond(
        crowded,
        lambda: dense_target(local, probs, voc_dev),
        lambda: compact_target(local, probs, voc_dev),
    )


def coords():
    tok = lax.axis_index("tok")
    voc = lax.axis_index("voc")
    return {"x": tok // RING, "y": tok % RING, "z": voc // 2, "c": voc % 2}


AXES = ("tok", "voc")


def device_coords(d, voc_n):
    tok, voc = divmod(d, voc_n)
    return tok // RING, tok % RING, voc // 2, voc % 2


def device_id(x, y, z, c, voc_n):
    return (x * RING + y) * voc_n + z * 2 + c


def ring_axis(stage, core):
    if stage == "r1":
        return "y"
    if stage == "r2":
        return "x" if core == 0 else "z"
    if stage == "r3":
        return "z" if core == 0 else "x"
    return stage


def stage_pairs(stage, shift, n_dev, voc_n):
    pairs = []
    for d in range(n_dev):
        x, y, z, c = device_coords(d, voc_n)
        axis = ring_axis(stage, c)
        if axis == "c":
            c = c ^ 1
        elif axis == "x":
            x = (x + shift) % RING
        elif axis == "y":
            y = (y + shift) % RING
        else:
            z = (z + shift) % RING
        pairs.append((d, device_id(x, y, z, c, voc_n)))
    return pairs


def exchange(block_for, stage, n_dev, voc_n):
    n = 2 if stage == "c" else RING
    got = [block_for(0)]
    for shift in range(1, n):
        got.append(lax.ppermute(block_for(shift), AXES, stage_pairs(stage, shift, n_dev, voc_n)))
    return jnp.stack(got)


def arrival_tokens(at):
    r = jnp.arange(2 * RING ** 3 * 4, dtype=jnp.int32)
    i = r % 4
    s_r1 = (r // 4) % RING
    s_r2 = (r // 16) % RING
    s_r3 = (r // 64) % RING
    c = at["c"] ^ (r // 256)
    s_x = jnp.where(c == 0, s_r2, s_r3)
    s_z = jnp.where(c == 0, s_r3, s_r2)
    x = (at["x"] - s_x) % RING
    y = (at["y"] - s_r1) % RING
    z = (at["z"] - s_z) % RING
    return (((x * RING + y) * RING + z) * 2 + c) * 4 + i


def natural_rows(at):
    t = jnp.arange(2 * RING ** 3 * 4, dtype=jnp.int32)
    i = t % 4
    c = (t // 4) % 2
    s_c = at["c"] ^ c
    s_z = (at["z"] - (t // 8) % RING) % RING
    s_y = (at["y"] - (t // 32) % RING) % RING
    s_x = (at["x"] - (t // 128) % RING) % RING
    s_r2 = jnp.where(c == 0, s_x, s_z)
    s_r3 = jnp.where(c == 0, s_z, s_x)
    return (((s_c * RING + s_r3) * RING + s_r2) * RING + s_y) * 4 + i


def half_logits(rows_block, head_weight):
    return lax.dot_general(
        rows_block, head_weight, (((1,), (1,)), ((), ())), preferred_element_type=jnp.float32
    )


def per_device(hidden_rows, head_weight, teacher_index, teacher_logprob, n_dev, voc_n):
    voc_dev = head_weight.shape[0]
    tok_dev = hidden_rows.shape[0]
    width = hidden_rows.shape[1]
    at = coords()

    position = lax.axis_index(("tok", "voc"))
    offset = position * voc_dev
    rows = arrival_tokens(at)
    index_arr = jnp.take(teacher_index, rows, axis=0)
    logprob_arr = jnp.take(teacher_logprob, rows, axis=0)
    local = index_arr - offset
    probs_arr = jnp.exp(logprob_arr)
    target = teacher_target(local, probs_arr, voc_dev)

    own = hidden_rows
    for stage in ("r1", "r2"):
        own = exchange(lambda s: own, stage, n_dev, voc_n).reshape(-1, width)
        if stage == "r2":
            own, target = lax.optimization_barrier((own, target))
    got = exchange(lambda s: own, "r3", n_dev, voc_n)
    first_logits = half_logits(own, head_weight)
    got, first_logits = lax.optimization_barrier((got, first_logits))
    own = got.reshape(-1, width)
    other = lax.ppermute(own, AXES, stage_pairs("c", 1, n_dev, voc_n))
    logits_own = jnp.concatenate(
        [first_logits, half_logits(got[1:].reshape(-1, width), head_weight)], axis=0
    )
    logits_other = half_logits(other, head_weight)
    every = jnp.concatenate([own, other], axis=0)
    half = own.shape[0]
    target_own, target_other = target[:half], target[half:]

    def local_stats(logits, tgt):
        peak = jnp.max(logits, axis=1)
        return peak, jnp.sum(jnp.exp(logits - peak[:, None]), axis=1), jnp.sum(logits * tgt, axis=1)

    own_stats = local_stats(logits_own, target_own)
    other_stats = local_stats(logits_other, target_other)
    stats = jnp.stack([jnp.concatenate([a, b]) for a, b in zip(own_stats, other_stats)])

    place = (rows[:, None] == jnp.arange(rows.shape[0], dtype=jnp.int32)[None, :]).astype(jnp.float32)
    stats = jnp.dot(stats, place, precision=lax.Precision.HIGHEST)
    for stage in ("c", "z", "y", "x"):
        got = exchange(lambda s: stats, stage, n_dev, voc_n)
        peak = jnp.max(got[:, 0], axis=0)
        summed = jnp.sum(got[:, 1] * jnp.exp(got[:, 0] - peak[None]), axis=0)
        dotted = jnp.sum(got[:, 2], axis=0)
        stats = jnp.stack([peak, summed, dotted])
    peak, summed, dotted = stats[0], stats[1], stats[2]

    lse = peak + jnp.log(summed)
    probs = jnp.exp(teacher_logprob)
    total_p = jnp.sum(probs, axis=1)
    own_term = jnp.sum(probs * teacher_logprob, axis=1)
    loss_all = own_term - dotted + total_p * lse
    row_loss = lax.dynamic_slice_in_dim(loss_all, position * tok_dev, tok_dev, 0)
    back = jnp.dot(place, jnp.stack([lse, total_p], axis=1), precision=lax.Precision.HIGHEST)
    lse_arr, total_arr = back[:, 0], back[:, 1]

    def half_grad(logits, tgt, lse_h, total_h):
        return (loss_scale * (total_h[:, None] * jnp.exp(logits - lse_h[:, None]) - tgt)).astype(
            jnp.bfloat16
        )

    grad_other = half_grad(logits_other, target_other, lse_arr[half:], total_arr[half:])

    sent = jnp.dot(grad_other, head_weight, preferred_element_type=jnp.float32).astype(jnp.bfloat16)
    received = lax.ppermute(sent, AXES, stage_pairs("c", 1, n_dev, voc_n))
    sent, logits_own = lax.optimization_barrier((sent, logits_own))
    grad_own = half_grad(logits_own, target_own, lse_arr[:half], total_arr[:half])
    acc = jnp.dot(grad_own, head_weight, preferred_element_type=jnp.float32)
    acc, received = lax.optimization_barrier((acc, received))
    acc = (acc + received.astype(jnp.float32)).reshape(RING, -1, width)
    grad = jnp.concatenate([grad_own, grad_other], axis=0)
    head_grad = lax.dot_general(
        grad, every, (((0,), (0,)), ((), ())), preferred_element_type=jnp.float32
    ).astype(jnp.bfloat16)
    for stage in ("r3", "r2", "r1"):
        got = exchange(lambda s: acc[(-s) % RING].astype(jnp.bfloat16), stage, n_dev, voc_n)
        acc = acc[0] + jnp.sum(got[1:].astype(jnp.float32), axis=0)
        if stage == "r3":
            acc, head_grad = lax.optimization_barrier((acc, head_grad))
        if stage != "r1":
            acc = acc.reshape(RING, -1, width)
    return (row_loss, head_grad, acc.astype(jnp.bfloat16))


def solution(mesh):
    voc_n = mesh.shape["voc"]
    n_dev = mesh.shape["tok"] * voc_n
    placed = (P(("tok", "voc"), None), P(("tok", "voc"), None), P(), P())

    def body(h, w, ti, tl):
        return per_device(h, w, ti, tl, n_dev, voc_n)

    return jax.shard_map(
        body,
        mesh=mesh,
        in_specs=placed,
        out_specs=(P(("tok", "voc")), P(("tok", "voc"), None), P(("tok", "voc"), None)),
        check_vma=False,
    )
```

```python
import jax
import jax.numpy as jnp
from jax import lax
from jax.sharding import PartitionSpec as P

loss_scale = 256.0
RING = 4


HITS = 8


def dense_target(local, probs, voc_dev):
    blocks = local.shape[0] // 64
    local_b = local.reshape(blocks, 64, local.shape[1])
    probs_b = probs.reshape(blocks, 64, probs.shape[1])
    columns = jnp.arange(voc_dev, dtype=jnp.int32)[None, None, :]

    def one_block(args):
        block_local, block_probs = args
        equal = block_local[:, :, None] == columns
        return jnp.sum(jnp.where(equal, block_probs[:, :, None], 0.0), axis=1)

    return lax.map(one_block, (local_b, probs_b)).reshape(local.shape[0], voc_dev)


def compact_target(local, probs, voc_dev):
    valid = (local >= 0) & (local < voc_dev)
    rank = jnp.cumsum(valid.astype(jnp.int32), axis=1) - 1
    slot = jnp.arange(HITS, dtype=jnp.int32)[None, None, :]
    chosen = valid[:, :, None] & (rank[:, :, None] == slot)
    slot_local = jnp.sum(jnp.where(chosen, local[:, :, None], 0), axis=1)
    slot_probs = jnp.sum(jnp.where(chosen, probs[:, :, None], 0.0), axis=1)
    columns = jnp.arange(voc_dev, dtype=jnp.int32)[None, :]
    target = jnp.zeros((local.shape[0], voc_dev), jnp.float32)
    for j in range(HITS):
        target = target + jnp.where(slot_local[:, j : j + 1] == columns, slot_probs[:, j : j + 1], 0.0)
    return target


def teacher_target(local, probs, voc_dev):
    valid = (local >= 0) & (local < voc_dev)
    crowded = jnp.any(jnp.sum(valid.astype(jnp.int32), axis=1) > HITS)
    return lax.cond(
        crowded,
        lambda: dense_target(local, probs, voc_dev),
        lambda: compact_target(local, probs, voc_dev),
    )


def coords():
    tok = lax.axis_index("tok")
    voc = lax.axis_index("voc")
    return {"x": tok // RING, "y": tok % RING, "z": voc // 2, "c": voc % 2}


AXES = ("tok", "voc")


def device_coords(d, voc_n):
    tok, voc = divmod(d, voc_n)
    return tok // RING, tok % RING, voc // 2, voc % 2


def device_id(x, y, z, c, voc_n):
    return (x * RING + y) * voc_n + z * 2 + c


def ring_axis(stage, core):
    if stage == "r1":
        return "y"
    if stage == "r2":
        return "x" if core == 0 else "z"
    if stage == "r3":
        return "z" if core == 0 else "x"
    return stage


def stage_pairs(stage, shift, n_dev, voc_n):
    pairs = []
    for d in range(n_dev):
        x, y, z, c = device_coords(d, voc_n)
        axis = ring_axis(stage, c)
        if axis == "c":
            c = c ^ 1
        elif axis == "x":
            x = (x + shift) % RING
        elif axis == "y":
            y = (y + shift) % RING
        else:
            z = (z + shift) % RING
        pairs.append((d, device_id(x, y, z, c, voc_n)))
    return pairs


def exchange(block_for, stage, n_dev, voc_n):
    n = 2 if stage == "c" else RING
    got = [block_for(0)]
    for shift in range(1, n):
        got.append(lax.ppermute(block_for(shift), AXES, stage_pairs(stage, shift, n_dev, voc_n)))
    return jnp.stack(got)


def arrival_tokens(at):
    r = jnp.arange(2 * RING ** 3 * 4, dtype=jnp.int32)
    i = r % 4
    s_r1 = (r // 4) % RING
    s_r2 = (r // 16) % RING
    s_r3 = (r // 64) % RING
    c = at["c"] ^ (r // 256)
    s_x = jnp.where(c == 0, s_r2, s_r3)
    s_z = jnp.where(c == 0, s_r3, s_r2)
    x = (at["x"] - s_x) % RING
    y = (at["y"] - s_r1) % RING
    z = (at["z"] - s_z) % RING
    return (((x * RING + y) * RING + z) * 2 + c) * 4 + i


def natural_rows(at):
    t = jnp.arange(2 * RING ** 3 * 4, dtype=jnp.int32)
    i = t % 4
    c = (t // 4) % 2
    s_c = at["c"] ^ c
    s_z = (at["z"] - (t // 8) % RING) % RING
    s_y = (at["y"] - (t // 32) % RING) % RING
    s_x = (at["x"] - (t // 128) % RING) % RING
    s_r2 = jnp.where(c == 0, s_x, s_z)
    s_r3 = jnp.where(c == 0, s_z, s_x)
    return (((s_c * RING + s_r3) * RING + s_r2) * RING + s_y) * 4 + i


def half_logits(rows_block, head_weight):
    return lax.dot_general(
        rows_block, head_weight, (((1,), (1,)), ((), ())), preferred_element_type=jnp.float32
    )


def per_device(hidden_rows, head_weight, teacher_index, teacher_logprob, n_dev, voc_n):
    voc_dev = head_weight.shape[0]
    tok_dev = hidden_rows.shape[0]
    width = hidden_rows.shape[1]
    at = coords()

    position = lax.axis_index(("tok", "voc"))
    offset = position * voc_dev
    rows = arrival_tokens(at)
    index_arr = jnp.take(teacher_index, rows, axis=0)
    logprob_arr = jnp.take(teacher_logprob, rows, axis=0)
    local = index_arr - offset
    probs_arr = jnp.exp(logprob_arr)
    target = teacher_target(local, probs_arr, voc_dev)

    own = hidden_rows
    for stage in ("r1", "r2"):
        own = exchange(lambda s: own, stage, n_dev, voc_n).reshape(-1, width)
        if stage == "r2":
            own, target = lax.optimization_barrier((own, target))
    got = exchange(lambda s: own, "r3", n_dev, voc_n)
    first_logits = half_logits(own, head_weight)
    got, first_logits = lax.optimization_barrier((got, first_logits))
    own = got.reshape(-1, width)
    other = lax.ppermute(own, AXES, stage_pairs("c", 1, n_dev, voc_n))
    logits_own = jnp.concatenate(
        [first_logits, half_logits(got[1:].reshape(-1, width), head_weight)], axis=0
    )
    half = own.shape[0]
    target_own, target_other = target[:half], target[half:]

    def local_stats(logits, tgt):
        peak = jnp.max(logits, axis=1)
        return peak, jnp.sum(jnp.exp(logits - peak[:, None]), axis=1), jnp.sum(logits * tgt, axis=1)

    own_stats = local_stats(logits_own, target_own)
    own_stats, other = lax.optimization_barrier((own_stats, other))
    logits_other = half_logits(other, head_weight)
    other_stats = local_stats(logits_other, target_other)
    stats = jnp.stack([jnp.concatenate([a, b]) for a, b in zip(own_stats, other_stats)])

    place = (rows[:, None] == jnp.arange(rows.shape[0], dtype=jnp.int32)[None, :]).astype(jnp.float32)
    stats = jnp.dot(stats, place, precision=lax.Precision.HIGHEST)
    for stage in ("c", "z", "y", "x"):
        got = exchange(lambda s: stats, stage, n_dev, voc_n)
        peak = jnp.max(got[:, 0], axis=0)
        summed = jnp.sum(got[:, 1] * jnp.exp(got[:, 0] - peak[None]), axis=0)
        dotted = jnp.sum(got[:, 2], axis=0)
        stats = jnp.stack([peak, summed, dotted])
    peak, summed, dotted = stats[0], stats[1], stats[2]

    lse = peak + jnp.log(summed)
    probs = jnp.exp(teacher_logprob)
    total_p = jnp.sum(probs, axis=1)
    own_term = jnp.sum(probs * teacher_logprob, axis=1)
    loss_all = own_term - dotted + total_p * lse
    row_loss = lax.dynamic_slice_in_dim(loss_all, position * tok_dev, tok_dev, 0)
    back = jnp.dot(place, jnp.stack([lse, total_p], axis=1), precision=lax.Precision.HIGHEST)
    lse_arr, total_arr = back[:, 0], back[:, 1]

    def half_grad(logits, tgt, lse_h, total_h):
        return (loss_scale * (total_h[:, None] * jnp.exp(logits - lse_h[:, None]) - tgt)).astype(
            jnp.bfloat16
        )

    grad_other = half_grad(logits_other, target_other, lse_arr[half:], total_arr[half:])

    sent = jnp.dot(grad_other, head_weight, preferred_element_type=jnp.float32).astype(jnp.bfloat16)
    received = lax.ppermute(sent, AXES, stage_pairs("c", 1, n_dev, voc_n))
    sent, logits_own = lax.optimization_barrier((sent, logits_own))
    grad_own = half_grad(logits_own, target_own, lse_arr[:half], total_arr[:half])
    acc = jnp.dot(grad_own, head_weight, preferred_element_type=jnp.float32)
    acc, received = lax.optimization_barrier((acc, received))
    acc = (acc + received.astype(jnp.float32)).reshape(RING, -1, width)
    every = jnp.concatenate([own, other], axis=0)
    grad = jnp.concatenate([grad_own, grad_other], axis=0)
    head_grad = lax.dot_general(
        grad, every, (((0,), (0,)), ((), ())), preferred_element_type=jnp.float32
    ).astype(jnp.bfloat16)
    for stage in ("r3", "r2", "r1"):
        got = exchange(lambda s: acc[(-s) % RING].astype(jnp.bfloat16), stage, n_dev, voc_n)
        acc = acc[0] + jnp.sum(got[1:].astype(jnp.float32), axis=0)
        if stage == "r3":
            acc, head_grad = lax.optimization_barrier((acc, head_grad))
        if stage != "r1":
            acc = acc.reshape(RING, -1, width)
    return (row_loss, head_grad, acc.astype(jnp.bfloat16))


def solution(mesh):
    voc_n = mesh.shape["voc"]
    n_dev = mesh.shape["tok"] * voc_n
    placed = (P(("tok", "voc"), None), P(("tok", "voc"), None), P(), P())

    def body(h, w, ti, tl):
        return per_device(h, w, ti, tl, n_dev, voc_n)

    return jax.shard_map(
        body,
        mesh=mesh,
        in_specs=placed,
        out_specs=(P(("tok", "voc")), P(("tok", "voc"), None), P(("tok", "voc"), None)),
        check_vma=False,
    )
```

```python
import jax
import jax.numpy as jnp
from jax import lax
from jax.sharding import PartitionSpec as P

loss_scale = 256.0
RING = 4


HITS = 8


def dense_target(local, probs, voc_dev):
    blocks = local.shape[0] // 64
    local_b = local.reshape(blocks, 64, local.shape[1])
    probs_b = probs.reshape(blocks, 64, probs.shape[1])
    columns = jnp.arange(voc_dev, dtype=jnp.int32)[None, None, :]

    def one_block(args):
        block_local, block_probs = args
        equal = block_local[:, :, None] == columns
        return jnp.sum(jnp.where(equal, block_probs[:, :, None], 0.0), axis=1)

    return lax.map(one_block, (local_b, probs_b)).reshape(local.shape[0], voc_dev)


def compact_target(local, probs, voc_dev):
    valid = (local >= 0) & (local < voc_dev)
    rank = jnp.cumsum(valid.astype(jnp.int32), axis=1) - 1
    slot = jnp.arange(HITS, dtype=jnp.int32)[None, None, :]
    chosen = valid[:, :, None] & (rank[:, :, None] == slot)
    slot_local = jnp.sum(jnp.where(chosen, local[:, :, None], 0), axis=1)
    slot_probs = jnp.sum(jnp.where(chosen, probs[:, :, None], 0.0), axis=1)
    columns = jnp.arange(voc_dev, dtype=jnp.int32)[None, :]
    target = jnp.zeros((local.shape[0], voc_dev), jnp.float32)
    for j in range(HITS):
        target = target + jnp.where(slot_local[:, j : j + 1] == columns, slot_probs[:, j : j + 1], 0.0)
    return target


def teacher_target(local, probs, voc_dev):
    valid = (local >= 0) & (local < voc_dev)
    crowded = jnp.any(jnp.sum(valid.astype(jnp.int32), axis=1) > HITS)
    return lax.cond(
        crowded,
        lambda: dense_target(local, probs, voc_dev),
        lambda: compact_target(local, probs, voc_dev),
    )


def coords():
    tok = lax.axis_index("tok")
    voc = lax.axis_index("voc")
    return {"x": tok // RING, "y": tok % RING, "z": voc // 2, "c": voc % 2}


AXES = ("tok", "voc")


def device_coords(d, voc_n):
    tok, voc = divmod(d, voc_n)
    return tok // RING, tok % RING, voc // 2, voc % 2


def device_id(x, y, z, c, voc_n):
    return (x * RING + y) * voc_n + z * 2 + c


def ring_axis(stage, core):
    if stage == "r1":
        return "y"
    if stage == "r2":
        return "x" if core == 0 else "z"
    if stage == "r3":
        return "z" if core == 0 else "x"
    return stage


def stage_pairs(stage, shift, n_dev, voc_n):
    pairs = []
    for d in range(n_dev):
        x, y, z, c = device_coords(d, voc_n)
        axis = ring_axis(stage, c)
        if axis == "v":
            z, c = divmod((z * 2 + c + shift) % voc_n, 2)
        elif axis == "c":
            c = c ^ 1
        elif axis == "x":
            x = (x + shift) % RING
        elif axis == "y":
            y = (y + shift) % RING
        else:
            z = (z + shift) % RING
        pairs.append((d, device_id(x, y, z, c, voc_n)))
    return pairs


def exchange(block_for, stage, n_dev, voc_n):
    n = {"c": 2, "v": voc_n}.get(stage, RING)
    got = [block_for(0)]
    for shift in range(1, n):
        got.append(lax.ppermute(block_for(shift), AXES, stage_pairs(stage, shift, n_dev, voc_n)))
    return jnp.stack(got)


def arrival_tokens(at):
    r = jnp.arange(2 * RING ** 3 * 4, dtype=jnp.int32)
    i = r % 4
    s_r1 = (r // 4) % RING
    s_r2 = (r // 16) % RING
    s_r3 = (r // 64) % RING
    c = at["c"] ^ (r // 256)
    s_x = jnp.where(c == 0, s_r2, s_r3)
    s_z = jnp.where(c == 0, s_r3, s_r2)
    x = (at["x"] - s_x) % RING
    y = (at["y"] - s_r1) % RING
    z = (at["z"] - s_z) % RING
    return (((x * RING + y) * RING + z) * 2 + c) * 4 + i


def natural_rows(at):
    t = jnp.arange(2 * RING ** 3 * 4, dtype=jnp.int32)
    i = t % 4
    c = (t // 4) % 2
    s_c = at["c"] ^ c
    s_z = (at["z"] - (t // 8) % RING) % RING
    s_y = (at["y"] - (t // 32) % RING) % RING
    s_x = (at["x"] - (t // 128) % RING) % RING
    s_r2 = jnp.where(c == 0, s_x, s_z)
    s_r3 = jnp.where(c == 0, s_z, s_x)
    return (((s_c * RING + s_r3) * RING + s_r2) * RING + s_y) * 4 + i


def half_logits(rows_block, head_weight):
    return lax.dot_general(
        rows_block, head_weight, (((1,), (1,)), ((), ())), preferred_element_type=jnp.float32
    )


def per_device(hidden_rows, head_weight, teacher_index, teacher_logprob, n_dev, voc_n):
    voc_dev = head_weight.shape[0]
    tok_dev = hidden_rows.shape[0]
    width = hidden_rows.shape[1]
    at = coords()

    position = lax.axis_index(("tok", "voc"))
    offset = position * voc_dev
    rows = arrival_tokens(at)
    index_arr = jnp.take(teacher_index, rows, axis=0)
    logprob_arr = jnp.take(teacher_logprob, rows, axis=0)
    local = index_arr - offset
    probs_arr = jnp.exp(logprob_arr)
    target = teacher_target(local, probs_arr, voc_dev)

    own = hidden_rows
    for stage in ("r1", "r2"):
        own = exchange(lambda s: own, stage, n_dev, voc_n).reshape(-1, width)
        if stage == "r2":
            own, target = lax.optimization_barrier((own, target))
    got = exchange(lambda s: own, "r3", n_dev, voc_n)
    first_logits = half_logits(own, head_weight)
    got, first_logits = lax.optimization_barrier((got, first_logits))
    own = got.reshape(-1, width)
    other = lax.ppermute(own, AXES, stage_pairs("c", 1, n_dev, voc_n))
    logits_own = jnp.concatenate(
        [first_logits, half_logits(got[1:].reshape(-1, width), head_weight)], axis=0
    )
    logits_other = half_logits(other, head_weight)
    every = jnp.concatenate([own, other], axis=0)
    half = own.shape[0]
    target_own, target_other = target[:half], target[half:]

    def local_stats(logits, tgt):
        peak = jnp.max(logits, axis=1)
        return peak, jnp.sum(jnp.exp(logits - peak[:, None]), axis=1), jnp.sum(logits * tgt, axis=1)

    own_stats = local_stats(logits_own, target_own)
    other_stats = local_stats(logits_other, target_other)
    stats = jnp.stack([jnp.concatenate([a, b]) for a, b in zip(own_stats, other_stats)])

    place = (rows[:, None] == jnp.arange(rows.shape[0], dtype=jnp.int32)[None, :]).astype(jnp.float32)
    stats = jnp.dot(stats, place, precision=lax.Precision.HIGHEST)
    for stage in ("v", "y", "x"):
        got = exchange(lambda s: stats, stage, n_dev, voc_n)
        peak = jnp.max(got[:, 0], axis=0)
        summed = jnp.sum(got[:, 1] * jnp.exp(got[:, 0] - peak[None]), axis=0)
        dotted = jnp.sum(got[:, 2], axis=0)
        stats = jnp.stack([peak, summed, dotted])
    peak, summed, dotted = stats[0], stats[1], stats[2]

    lse = peak + jnp.log(summed)
    probs = jnp.exp(teacher_logprob)
    total_p = jnp.sum(probs, axis=1)
    own_term = jnp.sum(probs * teacher_logprob, axis=1)
    loss_all = own_term - dotted + total_p * lse
    row_loss = lax.dynamic_slice_in_dim(loss_all, position * tok_dev, tok_dev, 0)
    back = jnp.dot(place, jnp.stack([lse, total_p], axis=1), precision=lax.Precision.HIGHEST)
    lse_arr, total_arr = back[:, 0], back[:, 1]

    def half_grad(logits, tgt, lse_h, total_h):
        return (loss_scale * (total_h[:, None] * jnp.exp(logits - lse_h[:, None]) - tgt)).astype(
            jnp.bfloat16
        )

    grad_other = half_grad(logits_other, target_other, lse_arr[half:], total_arr[half:])

    sent = jnp.dot(grad_other, head_weight, preferred_element_type=jnp.float32).astype(jnp.bfloat16)
    received = lax.ppermute(sent, AXES, stage_pairs("c", 1, n_dev, voc_n))
    sent, logits_own = lax.optimization_barrier((sent, logits_own))
    grad_own = half_grad(logits_own, target_own, lse_arr[:half], total_arr[:half])
    acc = jnp.dot(grad_own, head_weight, preferred_element_type=jnp.float32)
    acc, received = lax.optimization_barrier((acc, received))
    acc = (acc + received.astype(jnp.float32)).reshape(RING, -1, width)
    grad = jnp.concatenate([grad_own, grad_other], axis=0)
    head_grad = lax.dot_general(
        grad, every, (((0,), (0,)), ((), ())), preferred_element_type=jnp.float32
    ).astype(jnp.bfloat16)
    for stage in ("r3", "r2", "r1"):
        got = exchange(lambda s: acc[(-s) % RING].astype(jnp.bfloat16), stage, n_dev, voc_n)
        acc = acc[0] + jnp.sum(got[1:].astype(jnp.float32), axis=0)
        if stage == "r3":
            acc, head_grad = lax.optimization_barrier((acc, head_grad))
        if stage != "r1":
            acc = acc.reshape(RING, -1, width)
    return (row_loss, head_grad, acc.astype(jnp.bfloat16))


def solution(mesh):
    voc_n = mesh.shape["voc"]
    n_dev = mesh.shape["tok"] * voc_n
    placed = (P(("tok", "voc"), None), P(("tok", "voc"), None), P(), P())

    def body(h, w, ti, tl):
        return per_device(h, w, ti, tl, n_dev, voc_n)

    return jax.shard_map(
        body,
        mesh=mesh,
        in_specs=placed,
        out_specs=(P(("tok", "voc")), P(("tok", "voc"), None), P(("tok", "voc"), None)),
        check_vma=False,
    )
```

```python
import jax
import jax.numpy as jnp
from jax import lax
from jax.sharding import PartitionSpec as P

loss_scale = 256.0
RING = 4


HITS = 8


def dense_target(local, probs, voc_dev):
    blocks = local.shape[0] // 64
    local_b = local.reshape(blocks, 64, local.shape[1])
    probs_b = probs.reshape(blocks, 64, probs.shape[1])
    columns = jnp.arange(voc_dev, dtype=jnp.int32)[None, None, :]

    def one_block(args):
        block_local, block_probs = args
        equal = block_local[:, :, None] == columns
        return jnp.sum(jnp.where(equal, block_probs[:, :, None], 0.0), axis=1)

    return lax.map(one_block, (local_b, probs_b)).reshape(local.shape[0], voc_dev)


def compact_target(local, probs, voc_dev):
    valid = (local >= 0) & (local < voc_dev)
    rank = jnp.cumsum(valid.astype(jnp.int32), axis=1) - 1
    slot = jnp.arange(HITS, dtype=jnp.int32)[None, None, :]
    chosen = valid[:, :, None] & (rank[:, :, None] == slot)
    slot_local = jnp.sum(jnp.where(chosen, local[:, :, None], 0), axis=1)
    slot_probs = jnp.sum(jnp.where(chosen, probs[:, :, None], 0.0), axis=1)
    columns = jnp.arange(voc_dev, dtype=jnp.int32)[None, :]
    target = jnp.zeros((local.shape[0], voc_dev), jnp.float32)
    for j in range(HITS):
        target = target + jnp.where(slot_local[:, j : j + 1] == columns, slot_probs[:, j : j + 1], 0.0)
    return target


def teacher_target(local, probs, voc_dev):
    valid = (local >= 0) & (local < voc_dev)
    crowded = jnp.any(jnp.sum(valid.astype(jnp.int32), axis=1) > HITS)
    return lax.cond(
        crowded,
        lambda: dense_target(local, probs, voc_dev),
        lambda: compact_target(local, probs, voc_dev),
    )


def coords():
    tok = lax.axis_index("tok")
    voc = lax.axis_index("voc")
    return {"x": tok // RING, "y": tok % RING, "z": voc // 2, "c": voc % 2}


AXES = ("tok", "voc")


def device_coords(d, voc_n):
    tok, voc = divmod(d, voc_n)
    return tok // RING, tok % RING, voc // 2, voc % 2


def device_id(x, y, z, c, voc_n):
    return (x * RING + y) * voc_n + z * 2 + c


def ring_axis(stage, core):
    if stage == "r1":
        return "y"
    if stage == "r2":
        return "x" if core == 0 else "z"
    if stage == "r3":
        return "z" if core == 0 else "x"
    return stage


def stage_pairs(stage, shift, n_dev, voc_n):
    pairs = []
    for d in range(n_dev):
        x, y, z, c = device_coords(d, voc_n)
        axis = ring_axis(stage, c)
        if axis in ("x1", "x2", "y1", "y2", "z1", "z2"):
            bit = int(axis[1])
            x, y, z = (x ^ bit, y, z) if axis[0] == "x" else (x, y ^ bit, z) if axis[0] == "y" else (x, y, z ^ bit)
        elif axis == "c":
            c = c ^ 1
        elif axis == "x":
            x = (x + shift) % RING
        elif axis == "y":
            y = (y + shift) % RING
        else:
            z = (z + shift) % RING
        pairs.append((d, device_id(x, y, z, c, voc_n)))
    return pairs


def exchange(block_for, stage, n_dev, voc_n):
    n = 2 if (stage == "c" or stage[0] in "xyz" and stage[1:] in ("1", "2")) else RING
    got = [block_for(0)]
    for shift in range(1, n):
        got.append(lax.ppermute(block_for(shift), AXES, stage_pairs(stage, shift, n_dev, voc_n)))
    return jnp.stack(got)


def arrival_tokens(at):
    r = jnp.arange(2 * RING ** 3 * 4, dtype=jnp.int32)
    i = r % 4
    s_r1 = (r // 4) % RING
    s_r2 = (r // 16) % RING
    s_r3 = (r // 64) % RING
    c = at["c"] ^ (r // 256)
    s_x = jnp.where(c == 0, s_r2, s_r3)
    s_z = jnp.where(c == 0, s_r3, s_r2)
    x = (at["x"] - s_x) % RING
    y = (at["y"] - s_r1) % RING
    z = (at["z"] - s_z) % RING
    return (((x * RING + y) * RING + z) * 2 + c) * 4 + i


def natural_rows(at):
    t = jnp.arange(2 * RING ** 3 * 4, dtype=jnp.int32)
    i = t % 4
    c = (t // 4) % 2
    s_c = at["c"] ^ c
    s_z = (at["z"] - (t // 8) % RING) % RING
    s_y = (at["y"] - (t // 32) % RING) % RING
    s_x = (at["x"] - (t // 128) % RING) % RING
    s_r2 = jnp.where(c == 0, s_x, s_z)
    s_r3 = jnp.where(c == 0, s_z, s_x)
    return (((s_c * RING + s_r3) * RING + s_r2) * RING + s_y) * 4 + i


def half_logits(rows_block, head_weight):
    return lax.dot_general(
        rows_block, head_weight, (((1,), (1,)), ((), ())), preferred_element_type=jnp.float32
    )


def per_device(hidden_rows, head_weight, teacher_index, teacher_logprob, n_dev, voc_n):
    voc_dev = head_weight.shape[0]
    tok_dev = hidden_rows.shape[0]
    width = hidden_rows.shape[1]
    at = coords()

    position = lax.axis_index(("tok", "voc"))
    offset = position * voc_dev
    rows = arrival_tokens(at)
    index_arr = jnp.take(teacher_index, rows, axis=0)
    logprob_arr = jnp.take(teacher_logprob, rows, axis=0)
    local = index_arr - offset
    probs_arr = jnp.exp(logprob_arr)
    target = teacher_target(local, probs_arr, voc_dev)

    own = hidden_rows
    for stage in ("r1", "r2"):
        own = exchange(lambda s: own, stage, n_dev, voc_n).reshape(-1, width)
        if stage == "r2":
            own, target = lax.optimization_barrier((own, target))
    got = exchange(lambda s: own, "r3", n_dev, voc_n)
    first_logits = half_logits(own, head_weight)
    got, first_logits = lax.optimization_barrier((got, first_logits))
    own = got.reshape(-1, width)
    other = lax.ppermute(own, AXES, stage_pairs("c", 1, n_dev, voc_n))
    logits_own = jnp.concatenate(
        [first_logits, half_logits(got[1:].reshape(-1, width), head_weight)], axis=0
    )
    logits_other = half_logits(other, head_weight)
    every = jnp.concatenate([own, other], axis=0)
    half = own.shape[0]
    target_own, target_other = target[:half], target[half:]

    def local_stats(logits, tgt):
        peak = jnp.max(logits, axis=1)
        return peak, jnp.sum(jnp.exp(logits - peak[:, None]), axis=1), jnp.sum(logits * tgt, axis=1)

    own_stats = local_stats(logits_own, target_own)
    other_stats = local_stats(logits_other, target_other)
    stats = jnp.stack([jnp.concatenate([a, b]) for a, b in zip(own_stats, other_stats)])

    place = (rows[:, None] == jnp.arange(rows.shape[0], dtype=jnp.int32)[None, :]).astype(jnp.float32)
    stats = jnp.dot(stats, place, precision=lax.Precision.HIGHEST)
    for stage in ("c", "z1", "z2", "y1", "y2", "x1", "x2"):
        got = exchange(lambda s: stats, stage, n_dev, voc_n)
        peak = jnp.max(got[:, 0], axis=0)
        summed = jnp.sum(got[:, 1] * jnp.exp(got[:, 0] - peak[None]), axis=0)
        dotted = jnp.sum(got[:, 2], axis=0)
        stats = jnp.stack([peak, summed, dotted])
    peak, summed, dotted = stats[0], stats[1], stats[2]

    lse = peak + jnp.log(summed)
    probs = jnp.exp(teacher_logprob)
    total_p = jnp.sum(probs, axis=1)
    own_term = jnp.sum(probs * teacher_logprob, axis=1)
    loss_all = own_term - dotted + total_p * lse
    row_loss = lax.dynamic_slice_in_dim(loss_all, position * tok_dev, tok_dev, 0)
    back = jnp.dot(place, jnp.stack([lse, total_p], axis=1), precision=lax.Precision.HIGHEST)
    lse_arr, total_arr = back[:, 0], back[:, 1]

    def half_grad(logits, tgt, lse_h, total_h):
        return (loss_scale * (total_h[:, None] * jnp.exp(logits - lse_h[:, None]) - tgt)).astype(
            jnp.bfloat16
        )

    grad_other = half_grad(logits_other, target_other, lse_arr[half:], total_arr[half:])

    sent = jnp.dot(grad_other, head_weight, preferred_element_type=jnp.float32).astype(jnp.bfloat16)
    received = lax.ppermute(sent, AXES, stage_pairs("c", 1, n_dev, voc_n))
    sent, logits_own = lax.optimization_barrier((sent, logits_own))
    grad_own = half_grad(logits_own, target_own, lse_arr[:half], total_arr[:half])
    acc = jnp.dot(grad_own, head_weight, preferred_element_type=jnp.float32)
    acc, received = lax.optimization_barrier((acc, received))
    acc = (acc + received.astype(jnp.float32)).reshape(RING, -1, width)
    grad = jnp.concatenate([grad_own, grad_other], axis=0)
    head_grad = lax.dot_general(
        grad, every, (((0,), (0,)), ((), ())), preferred_element_type=jnp.float32
    ).astype(jnp.bfloat16)
    for stage in ("r3", "r2", "r1"):
        got = exchange(lambda s: acc[(-s) % RING].astype(jnp.bfloat16), stage, n_dev, voc_n)
        acc = acc[0] + jnp.sum(got[1:].astype(jnp.float32), axis=0)
        if stage == "r3":
            acc, head_grad = lax.optimization_barrier((acc, head_grad))
        if stage != "r1":
            acc = acc.reshape(RING, -1, width)
    return (row_loss, head_grad, acc.astype(jnp.bfloat16))


def solution(mesh):
    voc_n = mesh.shape["voc"]
    n_dev = mesh.shape["tok"] * voc_n
    placed = (P(("tok", "voc"), None), P(("tok", "voc"), None), P(), P())

    def body(h, w, ti, tl):
        return per_device(h, w, ti, tl, n_dev, voc_n)

    return jax.shard_map(
        body,
        mesh=mesh,
        in_specs=placed,
        out_specs=(P(("tok", "voc")), P(("tok", "voc"), None), P(("tok", "voc"), None)),
        check_vma=False,
    )
```

```python
import jax
import jax.numpy as jnp
from jax import lax
from jax.sharding import PartitionSpec as P

loss_scale = 256.0
RING = 4


HITS = 8


def dense_target(local, probs, voc_dev):
    blocks = local.shape[0] // 64
    local_b = local.reshape(blocks, 64, local.shape[1])
    probs_b = probs.reshape(blocks, 64, probs.shape[1])
    columns = jnp.arange(voc_dev, dtype=jnp.int32)[None, None, :]

    def one_block(args):
        block_local, block_probs = args
        equal = block_local[:, :, None] == columns
        return jnp.sum(jnp.where(equal, block_probs[:, :, None], 0.0), axis=1)

    return lax.map(one_block, (local_b, probs_b)).reshape(local.shape[0], voc_dev)


def compact_target(local, probs, voc_dev):
    valid = (local >= 0) & (local < voc_dev)
    rank = jnp.cumsum(valid.astype(jnp.int32), axis=1) - 1
    slot = jnp.arange(HITS, dtype=jnp.int32)[None, None, :]
    chosen = valid[:, :, None] & (rank[:, :, None] == slot)
    slot_local = jnp.sum(jnp.where(chosen, local[:, :, None], 0), axis=1)
    slot_probs = jnp.sum(jnp.where(chosen, probs[:, :, None], 0.0), axis=1)
    columns = jnp.arange(voc_dev, dtype=jnp.int32)[None, :]
    target = jnp.zeros((local.shape[0], voc_dev), jnp.float32)
    for j in range(HITS):
        target = target + jnp.where(slot_local[:, j : j + 1] == columns, slot_probs[:, j : j + 1], 0.0)
    return target


def teacher_target(local, probs, voc_dev):
    valid = (local >= 0) & (local < voc_dev)
    crowded = jnp.any(jnp.sum(valid.astype(jnp.int32), axis=1) > HITS)
    return lax.cond(
        crowded,
        lambda: dense_target(local, probs, voc_dev),
        lambda: compact_target(local, probs, voc_dev),
    )


def coords():
    tok = lax.axis_index("tok")
    voc = lax.axis_index("voc")
    return {"x": tok // RING, "y": tok % RING, "z": voc // 2, "c": voc % 2}


AXES = ("tok", "voc")


def device_coords(d, voc_n):
    tok, voc = divmod(d, voc_n)
    return tok // RING, tok % RING, voc // 2, voc % 2


def device_id(x, y, z, c, voc_n):
    return (x * RING + y) * voc_n + z * 2 + c


def ring_axis(stage, core):
    if stage == "r1":
        return "y"
    if stage == "r2":
        return "x" if core == 0 else "z"
    if stage == "r3":
        return "z" if core == 0 else "x"
    return stage


def stage_pairs(stage, shift, n_dev, voc_n):
    pairs = []
    for d in range(n_dev):
        x, y, z, c = device_coords(d, voc_n)
        axis = ring_axis(stage, c)
        if axis == "c":
            c = c ^ 1
        elif axis == "x":
            x = (x + shift) % RING
        elif axis == "y":
            y = (y + shift) % RING
        else:
            z = (z + shift) % RING
        pairs.append((d, device_id(x, y, z, c, voc_n)))
    return pairs


def exchange(block_for, stage, n_dev, voc_n):
    n = 2 if stage == "c" else RING
    got = [block_for(0)]
    for shift in range(1, n):
        got.append(lax.ppermute(block_for(shift), AXES, stage_pairs(stage, shift, n_dev, voc_n)))
    return jnp.stack(got)


def arrival_tokens(at):
    r = jnp.arange(2 * RING ** 3 * 4, dtype=jnp.int32)
    i = r % 4
    s_r1 = (r // 4) % RING
    s_r2 = (r // 16) % RING
    s_r3 = (r // 64) % RING
    c = at["c"] ^ (r // 256)
    s_x = jnp.where(c == 0, s_r2, s_r3)
    s_z = jnp.where(c == 0, s_r3, s_r2)
    x = (at["x"] - s_x) % RING
    y = (at["y"] - s_r1) % RING
    z = (at["z"] - s_z) % RING
    return (((x * RING + y) * RING + z) * 2 + c) * 4 + i


def natural_rows(at):
    t = jnp.arange(2 * RING ** 3 * 4, dtype=jnp.int32)
    i = t % 4
    c = (t // 4) % 2
    s_c = at["c"] ^ c
    s_z = (at["z"] - (t // 8) % RING) % RING
    s_y = (at["y"] - (t // 32) % RING) % RING
    s_x = (at["x"] - (t // 128) % RING) % RING
    s_r2 = jnp.where(c == 0, s_x, s_z)
    s_r3 = jnp.where(c == 0, s_z, s_x)
    return (((s_c * RING + s_r3) * RING + s_r2) * RING + s_y) * 4 + i


def half_logits(rows_block, head_weight):
    return lax.dot_general(
        rows_block, head_weight, (((1,), (1,)), ((), ())), preferred_element_type=jnp.float32
    )


def per_device(hidden_rows, head_weight, teacher_index, teacher_logprob, n_dev, voc_n):
    voc_dev = head_weight.shape[0]
    tok_dev = hidden_rows.shape[0]
    width = hidden_rows.shape[1]
    at = coords()

    position = lax.axis_index(("tok", "voc"))
    offset = position * voc_dev
    rows = arrival_tokens(at)
    index_arr = jnp.take(teacher_index, rows, axis=0)
    logprob_arr = jnp.take(teacher_logprob, rows, axis=0)
    local = index_arr - offset
    probs_arr = jnp.exp(logprob_arr)

    own = hidden_rows
    for stage in ("r1", "r2"):
        own = exchange(lambda s: own, stage, n_dev, voc_n).reshape(-1, width)
    own, local, probs_arr = lax.optimization_barrier((own, local, probs_arr))
    got = exchange(lambda s: own, "r3", n_dev, voc_n)
    target = teacher_target(local, probs_arr, voc_dev)
    first_logits = half_logits(own, head_weight)
    got, target, first_logits = lax.optimization_barrier((got, target, first_logits))
    own = got.reshape(-1, width)
    other = lax.ppermute(own, AXES, stage_pairs("c", 1, n_dev, voc_n))
    logits_own = jnp.concatenate(
        [first_logits, half_logits(got[1:].reshape(-1, width), head_weight)], axis=0
    )
    logits_other = half_logits(other, head_weight)
    every = jnp.concatenate([own, other], axis=0)
    half = own.shape[0]
    target_own, target_other = target[:half], target[half:]

    def local_stats(logits, tgt):
        peak = jnp.max(logits, axis=1)
        return peak, jnp.sum(jnp.exp(logits - peak[:, None]), axis=1), jnp.sum(logits * tgt, axis=1)

    own_stats = local_stats(logits_own, target_own)
    other_stats = local_stats(logits_other, target_other)
    stats = jnp.stack([jnp.concatenate([a, b]) for a, b in zip(own_stats, other_stats)])

    place = (rows[:, None] == jnp.arange(rows.shape[0], dtype=jnp.int32)[None, :]).astype(jnp.float32)
    stats = jnp.dot(stats, place, precision=lax.Precision.HIGHEST)
    for stage in ("c", "z", "y", "x"):
        got = exchange(lambda s: stats, stage, n_dev, voc_n)
        peak = jnp.max(got[:, 0], axis=0)
        summed = jnp.sum(got[:, 1] * jnp.exp(got[:, 0] - peak[None]), axis=0)
        dotted = jnp.sum(got[:, 2], axis=0)
        stats = jnp.stack([peak, summed, dotted])
    peak, summed, dotted = stats[0], stats[1], stats[2]

    lse = peak + jnp.log(summed)
    probs = jnp.exp(teacher_logprob)
    total_p = jnp.sum(probs, axis=1)
    own_term = jnp.sum(probs * teacher_logprob, axis=1)
    loss_all = own_term - dotted + total_p * lse
    row_loss = lax.dynamic_slice_in_dim(loss_all, position * tok_dev, tok_dev, 0)
    back = jnp.dot(place, jnp.stack([lse, total_p], axis=1), precision=lax.Precision.HIGHEST)
    lse_arr, total_arr = back[:, 0], back[:, 1]

    def half_grad(logits, tgt, lse_h, total_h):
        return (loss_scale * (total_h[:, None] * jnp.exp(logits - lse_h[:, None]) - tgt)).astype(
            jnp.bfloat16
        )

    grad_other = half_grad(logits_other, target_other, lse_arr[half:], total_arr[half:])

    sent = jnp.dot(grad_other, head_weight, preferred_element_type=jnp.float32).astype(jnp.bfloat16)
    received = lax.ppermute(sent, AXES, stage_pairs("c", 1, n_dev, voc_n))
    sent, logits_own = lax.optimization_barrier((sent, logits_own))
    grad_own = half_grad(logits_own, target_own, lse_arr[:half], total_arr[:half])
    acc = jnp.dot(grad_own, head_weight, preferred_element_type=jnp.float32)
    acc, received = lax.optimization_barrier((acc, received))
    acc = (acc + received.astype(jnp.float32)).reshape(RING, -1, width)
    grad = jnp.concatenate([grad_own, grad_other], axis=0)
    head_grad = lax.dot_general(
        grad, every, (((0,), (0,)), ((), ())), preferred_element_type=jnp.float32
    ).astype(jnp.bfloat16)
    for stage in ("r3", "r2", "r1"):
        got = exchange(lambda s: acc[(-s) % RING].astype(jnp.bfloat16), stage, n_dev, voc_n)
        acc = acc[0] + jnp.sum(got[1:].astype(jnp.float32), axis=0)
        if stage == "r3":
            acc, head_grad = lax.optimization_barrier((acc, head_grad))
        if stage != "r1":
            acc = acc.reshape(RING, -1, width)
    return (row_loss, head_grad, acc.astype(jnp.bfloat16))


def solution(mesh):
    voc_n = mesh.shape["voc"]
    n_dev = mesh.shape["tok"] * voc_n
    placed = (P(("tok", "voc"), None), P(("tok", "voc"), None), P(), P())

    def body(h, w, ti, tl):
        return per_device(h, w, ti, tl, n_dev, voc_n)

    return jax.shard_map(
        body,
        mesh=mesh,
        in_specs=placed,
        out_specs=(P(("tok", "voc")), P(("tok", "voc"), None), P(("tok", "voc"), None)),
        check_vma=False,
    )
```
